32 devices in a mesh: test: 4 (over z), cell: 8 (over y, x, core).
Axes of the slice: x: 2, y: 2, z: 4, core: 2. Of those that a mesh axis runs over, the one named last changes fastest.
Arguments:
- log_perm: float32 [128, 16, 256], P('cell'), may hold values from -1 to 1
- panel: float32 [8, 128, 16, 256], P('test', 'cell'), may hold values from -4 to 4
- wells: int32 [4, 8], P('test'), may hold values from 0 to 524287
- rates: float32 [4, 8], P('test'), may hold values from 1 to 10
- recharge: float32 [4, 128, 16, 256], P('test', 'cell'), may hold values from 0.25 to 4
- gauge: float32 [128, 16, 256], P('cell'), may hold values from 0.25 to 4
Outputs:
- hessian_panel: float32 [8, 128, 16, 256], P('test', 'cell')
The draws below stay inside these ranges and needn't reach their ends.
Inputs may be any that keep to these rules, and one draw needn't show every extreme that they name: `wells`: each entry names a cell of the whole grid, numbered x * 16 * 256 + y * 256 + z; a test may name a cell more than once.
All inputs are finite; a program needn't handle non-finite values.
Results may differ from the reference program's by a relative error of at most 0.0001.
Values sent between devices are 32-bit elements; how exact they have to be, the bound alone decides.
No kernel may reach another device: no remote copies, remote signals or barrier semaphores. Data moves between devices by JAX's collectives and lax.ppermute only.
A program may use at most 64 MiB of HBM per device.

```python
import math
import jax
import jax.numpy as jnp
from jax import lax

NY = 16
NZ = 256
PANEL = 8
WELLS = 8
CHEB = 4
NX = 128
TESTS = 4


def plant(drawn, stream_key, least, largest):
    shape = drawn.shape
    place = [jax.random.randint(jax.random.fold_in(stream_key, axis), (), 0, shape[axis]) for axis in range(len(shape))]
    drawn = drawn.at[tuple(place)].set(least)
    longest = shape.index(max(shape))
    place[longest] = (place[longest] + 1) % shape[longest]
    return drawn.at[tuple(place)].set(largest)


def block_levels(own_key, dims, cuts, least, high):
    gain, own = 1.0, jax.random.fold_in(own_key, 6)
    for position, shards_of in cuts:
        draws = jnp.exp(jax.random.uniform(jax.random.fold_in(own, position), (shards_of,), jnp.float32, least / len(cuts), high / len(cuts)))
        gain = gain * jnp.repeat(draws, dims[position] // shards_of).reshape([-1 if axis == position else 1 for axis in range(len(dims))])
    return gain


def bell_draw(key, dims, scale, reach, cuts=(), dtype=jnp.bfloat16):
    loudness = block_levels(key, dims, cuts, -0.22, 0.18) if cuts else 1.0
    values = jax.random.normal(key, dims, jnp.float32) * scale * loudness
    return jnp.minimum(jnp.maximum(values, -reach), reach).astype(dtype)


def setup_inputs(seed: int = 0) -> dict:
    key_of = jax.random.split(jax.random.key(seed), 7)
    return {
        "log_perm": jnp.clip(jax.random.uniform(key_of[0], (NX, NY, NZ), jnp.float32, -1.0, 1.0) * block_levels(key_of[0], (NX, NY, NZ), ((0, 8),), -0.4, 0.0), -1.0, 1.0),
        "panel": bell_draw(key_of[1], (PANEL, NX, NY, NZ), 1.0, 4.0, ((0, 4), (1, 8)), jnp.float32),
        "wells": plant(jax.random.randint(key_of[2], (TESTS, WELLS), 0, NX * NY * NZ), jax.random.fold_in(key_of[2], 1), 0, (NX * NY * NZ) - 1).astype(jnp.int32),
        "rates": jnp.clip(jnp.exp(math.log(10.0) - 2.3025851 * jax.random.uniform(key_of[3], (TESTS, WELLS), jnp.float32) ** block_levels(key_of[3], (TESTS, WELLS), ((0, 4),), -0.2, 0.2)), 1.0, 10.0),
        "recharge": jnp.clip(jnp.exp(math.log(4.0) - 2.7725887 * jax.random.uniform(key_of[4], (TESTS, NX, NY, NZ), jnp.float32) ** block_levels(key_of[4], (TESTS, NX, NY, NZ), ((0, 4), (1, 8)), -0.2, 0.2)), 0.25, 4.0),
        "gauge": jnp.clip(jnp.exp(math.log(4.0) - 2.7725887 * jax.random.uniform(key_of[5], (NX, NY, NZ), jnp.float32) ** block_levels(key_of[5], (NX, NY, NZ), ((0, 8),), -0.2, 0.2)), 0.25, 4.0),
    }


storage = 0.02


def cheb_table(count):
    lowest = storage
    highest = storage + 12.0 * math.e
    theta = 0.5 * (highest + lowest)
    spread = 0.5 * (highest - lowest)
    sigma = theta / spread
    rho = 1.0 / sigma
    keeps = []
    pushes = []
    for turn in range(count):
        after = 1.0 / (2.0 * sigma - rho)
        keeps.append(after * rho)
        pushes.append(2.0 * after / spread)
        rho = after
    return 1.0 / theta, keeps, pushes


def neighbours(field, back):
    axis = field.ndim - back
    widths = [(0, 0)] * field.ndim
    widths[axis] = (1, 1)
    padded = jnp.pad(field, widths)
    length = field.shape[axis]
    return lax.slice_in_dim(padded, 2, length + 2, axis=axis), lax.slice_in_dim(padded, 0, length, axis=axis)


def pad_rows(field):
    widths = [(0, 0)] * field.ndim
    widths[field.ndim - 3] = (1, 1)
    return jnp.pad(field, widths)


def diffuse(weight_ext, field_ext):
    weight = weight_ext[..., 1:-1, :, :]
    field = field_ext[..., 1:-1, :, :]
    total = 0.5 * (weight + weight_ext[..., 2:, :, :]) * (field - field_ext[..., 2:, :, :])
    total = total + 0.5 * (weight + weight_ext[..., :-2, :, :]) * (field - field_ext[..., :-2, :, :])
    for back in (2, 1):
        weight_up, weight_down = neighbours(weight, back)
        field_up, field_down = neighbours(field, back)
        total = total + 0.5 * (weight + weight_up) * (field - field_up) + 0.5 * (weight + weight_down) * (field - field_down)
    return total


def pairs(left_ext, right_ext):
    left = left_ext[..., 1:-1, :, :]
    right = right_ext[..., 1:-1, :, :]
    total = (left - left_ext[..., 2:, :, :]) * (right - right_ext[..., 2:, :, :])
    total = total + (left - left_ext[..., :-2, :, :]) * (right - right_ext[..., :-2, :, :])
    for back in (2, 1):
        left_up, left_down = neighbours(left, back)
        right_up, right_down = neighbours(right, back)
        total = total + (left - left_up) * (right - right_up) + (left - left_down) * (right - right_down)
    return total


def reference(log_perm, panel, wells, rates, recharge, gauge):
    perm = jnp.exp(log_perm)
    perm_pad = pad_rows(perm)
    scaled_pad = pad_rows(perm[None] * panel)
    first, keeps, pushes = cheb_table(CHEB)

    def solve(source):
        solution = jnp.zeros_like(source)
        residual = source
        direction = source * first
        for turn in range(CHEB):
            solution = solution + direction
            image = storage * direction + diffuse(perm_pad, pad_rows(direction))
            residual = residual - image
            direction = keeps[turn] * direction + pushes[turn] * residual
        return solution + direction

    def per_test(carry, inputs):
        well_row, rate_row, recharge_row = inputs
        points = jnp.zeros((NX * NY * NZ,), jnp.float32).at[well_row].add(rate_row).reshape(NX, NY, NZ)
        counts = jnp.zeros((NX * NY * NZ,), jnp.float32).at[well_row].add(jnp.ones_like(rate_row)).reshape(NX, NY, NZ)
        source = recharge_row + points
        observe = gauge + counts
        state = solve(source)
        state_pad = pad_rows(state)
        forcing = -diffuse(scaled_pad, state_pad[None])
        change = solve(forcing)
        adjoint = solve(observe[None] * change)
        return carry + pairs(state_pad[None], pad_rows(adjoint)), None

    start = jnp.zeros((PANEL, NX, NY, NZ), jnp.float32)
    total, unused = lax.scan(per_test, start, (wells.astype(jnp.int32), rates, recharge))
    return -0.5 * perm[None] * total
```

```python
import math

import jax
import jax.numpy as jnp
from jax import lax
from jax.sharding import PartitionSpec as P

CHEB = 4


storage = 0.02


def with_halo(cells, axis, dim, width):
    count = lax.axis_size(axis)
    ends = count - 1
    head = lax.slice_in_dim(cells, 0, width, axis=dim)
    tail = lax.slice_in_dim(cells, cells.shape[dim] - width, cells.shape[dim], axis=dim)
    return jnp.concatenate(
        [
            lax.ppermute(tail, axis, [(i, i + 1) for i in range(ends)]),
            cells,
            lax.ppermute(head, axis, [(i + 1, i) for i in range(ends)]),
        ],
        axis=dim,
    )


def cheb_table(count):
    highest = storage + 12.0 * math.e
    theta = 0.5 * (highest + storage)
    spread = 0.5 * (highest - storage)
    sigma = theta / spread
    rho = 1.0 / sigma
    keeps = []
    pushes = []
    for turn in range(count):
        after = 1.0 / (2.0 * sigma - rho)
        keeps.append(after * rho)
        pushes.append(2.0 * after / spread)
        rho = after
    return (1.0 / theta, keeps, pushes)


def neighbours(field, back):
    axis = field.ndim - back
    widths = [(0, 0)] * field.ndim
    widths[axis] = (1, 1)
    padded = jnp.pad(field, widths)
    length = field.shape[axis]
    return (
        lax.slice_in_dim(padded, 2, length + 2, axis=axis),
        lax.slice_in_dim(padded, 0, length, axis=axis),
    )


def diffuse(weight_ext, field_ext):
    weight = weight_ext[..., 1:-1, :, :]
    field = field_ext[..., 1:-1, :, :]
    total = 0.5 * (weight + weight_ext[..., 2:, :, :]) * (field - field_ext[..., 2:, :, :])
    total = total + 0.5 * (weight + weight_ext[..., :-2, :, :]) * (
        field - field_ext[..., :-2, :, :]
    )
    for back in (2, 1):
        weight_up, weight_down = neighbours(weight, back)
        field_up, field_down = neighbours(field, back)
        total = (
            total
            + 0.5 * (weight + weight_up) * (field - field_up)
            + 0.5 * (weight + weight_down) * (field - field_down)
        )
    return total


def pairs(left_ext, right_ext):
    left = left_ext[..., 1:-1, :, :]
    right = right_ext[..., 1:-1, :, :]
    total = (left - left_ext[..., 2:, :, :]) * (right - right_ext[..., 2:, :, :])
    total = total + (left - left_ext[..., :-2, :, :]) * (right - right_ext[..., :-2, :, :])
    for back in (2, 1):
        left_up, left_down = neighbours(left, back)
        right_up, right_down = neighbours(right, back)
        total = (
            total
            + (left - left_up) * (right - right_up)
            + (left - left_down) * (right - right_down)
        )
    return total


def inner(field):
    return field[..., 1:-1, :, :]


def shards(log_perm, panel, wells, rates, recharge, gauge):
    place = lax.axis_index("cell")
    parts = lax.axis_size("cell")
    slab, rows_y, depth_z = log_perm.shape
    cols = panel.shape[0]
    first, keeps, pushes = cheb_table(CHEB)
    reach = 5
    perm = jnp.exp(log_perm)
    scaled = perm[None] * panel
    rech = lax.all_gather(recharge, "test", axis=0, tiled=True)
    wells_all = lax.all_gather(wells, "test", axis=0, tiled=True)
    rates_all = lax.all_gather(rates, "test", axis=0, tiled=True)
    tests = rech.shape[0]
    stacked = jnp.concatenate([perm[None], scaled, rech], axis=0)
    ext = with_halo(stacked, "cell", 1, reach)
    perm_ext = ext[0]
    scaled_ext = ext[1 : 1 + cols]
    rech_ext = ext[1 + cols :]
    rows_ext = slab + 2 * reach
    gx = place * slab - reach + jnp.arange(rows_ext, dtype=jnp.int32)
    mask_ext = ((gx >= 0) & (gx < parts * slab)).astype(jnp.float32)[:, None, None]
    flat = (
        gx[:, None, None] * (rows_y * depth_z)
        + jnp.arange(rows_y, dtype=jnp.int32)[None, :, None] * depth_z
        + jnp.arange(depth_z, dtype=jnp.int32)[None, None, :]
    )
    hits = wells_all[:, :, None, None, None] == flat[None, None]
    points = jnp.sum(jnp.where(hits, rates_all[:, :, None, None, None], 0.0), axis=1)
    own_hits = hits[:, :, reach : reach + slab]
    counts = jnp.sum(own_hits.astype(jnp.float32), axis=1)
    source_ext = rech_ext + points
    observe = gauge[None] + counts

    def rows_of(field, halo):
        return lax.slice_in_dim(field, reach - halo, reach + slab + halo, axis=field.ndim - 3)

    def solve(right_side, halo):
        solution = jnp.zeros_like(right_side)
        residual = right_side
        direction = right_side * first
        for turn in range(CHEB):
            weight = rows_of(perm_ext, halo)
            image = storage * inner(direction) + diffuse(weight, direction)
            solution = inner(solution) + inner(direction)
            residual = inner(residual) - image
            halo -= 1
            direction = (keeps[turn] * inner(direction) + pushes[turn] * residual) * rows_of(
                mask_ext, halo
            )
        return solution + direction, halo

    state, state_halo = solve(source_ext, reach)
    forcing = -diffuse(rows_of(scaled_ext, state_halo)[None], state[:, None])
    forcing = forcing.reshape(tests * cols, slab, rows_y, depth_z)
    forcing_ext = with_halo(forcing, "cell", 1, CHEB)
    change, _ = solve(forcing_ext, CHEB)
    weighted = (
        change.reshape(tests, cols, slab, rows_y, depth_z) * observe[:, None]
    ).reshape(tests * cols, slab, rows_y, depth_z)
    weighted_ext = with_halo(weighted, "cell", 1, CHEB + 1)
    adjoint, _ = solve(weighted_ext, CHEB + 1)
    adjoint = adjoint.reshape(tests, cols, slab + 2, rows_y, depth_z)
    contrib = jnp.sum(pairs(state[:, None], adjoint), axis=0)
    return -0.5 * perm[None] * contrib


def solution(mesh):
    return jax.shard_map(
        shards,
        mesh=mesh,
        in_specs=(
            P("cell", None, None),
            P("test", "cell", None, None),
            P("test", None),
            P("test", None),
            P("test", "cell", None, None),
            P("cell", None, None),
        ),
        out_specs=P("test", "cell", None, None),
        check_vma=False,
    )
```

```python
import math

import jax
import jax.numpy as jnp
from jax import lax
from jax.sharding import PartitionSpec as P

CHEB = 4


storage = 0.02


def with_halo(cells, axis, dim, width):
    count = lax.axis_size(axis)
    ends = count - 1
    head = lax.slice_in_dim(cells, 0, width, axis=dim)
    tail = lax.slice_in_dim(cells, cells.shape[dim] - width, cells.shape[dim], axis=dim)
    return jnp.concatenate(
        [
            lax.ppermute(tail, axis, [(i, i + 1) for i in range(ends)]),
            cells,
            lax.ppermute(head, axis, [(i + 1, i) for i in range(ends)]),
        ],
        axis=dim,
    )


def cheb_table(count):
    highest = storage + 12.0 * math.e
    theta = 0.5 * (highest + storage)
    spread = 0.5 * (highest - storage)
    sigma = theta / spread
    rho = 1.0 / sigma
    keeps = []
    pushes = []
    for turn in range(count):
        after = 1.0 / (2.0 * sigma - rho)
        keeps.append(after * rho)
        pushes.append(2.0 * after / spread)
        rho = after
    return (1.0 / theta, keeps, pushes)


def neighbours(field, back):
    axis = field.ndim - back
    widths = [(0, 0)] * field.ndim
    widths[axis] = (1, 1)
    padded = jnp.pad(field, widths)
    length = field.shape[axis]
    return (
        lax.slice_in_dim(padded, 2, length + 2, axis=axis),
        lax.slice_in_dim(padded, 0, length, axis=axis),
    )


def diffuse(weight_ext, field_ext):
    weight = weight_ext[..., 1:-1, :, :]
    field = field_ext[..., 1:-1, :, :]
    total = 0.5 * (weight + weight_ext[..., 2:, :, :]) * (field - field_ext[..., 2:, :, :])
    total = total + 0.5 * (weight + weight_ext[..., :-2, :, :]) * (
        field - field_ext[..., :-2, :, :]
    )
    for back in (2, 1):
        weight_up, weight_down = neighbours(weight, back)
        field_up, field_down = neighbours(field, back)
        total = (
            total
            + 0.5 * (weight + weight_up) * (field - field_up)
            + 0.5 * (weight + weight_down) * (field - field_down)
        )
    return total


def pairs(left_ext, right_ext):
    left = left_ext[..., 1:-1, :, :]
    right = right_ext[..., 1:-1, :, :]
    total = (left - left_ext[..., 2:, :, :]) * (right - right_ext[..., 2:, :, :])
    total = total + (left - left_ext[..., :-2, :, :]) * (right - right_ext[..., :-2, :, :])
    for back in (2, 1):
        left_up, left_down = neighbours(left, back)
        right_up, right_down = neighbours(right, back)
        total = (
            total
            + (left - left_up) * (right - right_up)
            + (left - left_down) * (right - right_down)
        )
    return total


def inner(field):
    return field[..., 1:-1, :, :]


def shards(log_perm, panel, wells, rates, recharge, gauge):
    place = lax.axis_index("cell")
    parts = lax.axis_size("cell")
    slab, rows_y, depth_z = log_perm.shape
    cols = panel.shape[0]
    first, keeps, pushes = cheb_table(CHEB)
    reach = 5
    perm = jnp.exp(log_perm)
    scaled = perm[None] * panel
    tests_here, well_count = wells.shape
    cells = slab * rows_y * depth_z
    packed = jnp.concatenate(
        [recharge.reshape(tests_here, cells), wells.astype(jnp.float32), rates], axis=1
    )
    packed = lax.all_gather(packed, "test", axis=0, tiled=True)
    tests = packed.shape[0]
    rech = packed[:, :cells].reshape(tests, slab, rows_y, depth_z)
    wells_all = packed[:, cells : cells + well_count].astype(jnp.int32)
    rates_all = packed[:, cells + well_count :]
    stacked = jnp.concatenate([perm[None], scaled, rech], axis=0)
    ext = with_halo(stacked, "cell", 1, reach)
    perm_ext = ext[0]
    scaled_ext = ext[1 : 1 + cols]
    rech_ext = ext[1 + cols :]
    rows_ext = slab + 2 * reach
    gx = place * slab - reach + jnp.arange(rows_ext, dtype=jnp.int32)
    mask_ext = ((gx >= 0) & (gx < parts * slab)).astype(jnp.float32)[:, None, None]
    flat = (
        gx[:, None, None] * (rows_y * depth_z)
        + jnp.arange(rows_y, dtype=jnp.int32)[None, :, None] * depth_z
        + jnp.arange(depth_z, dtype=jnp.int32)[None, None, :]
    )
    hits = wells_all[:, :, None, None, None] == flat[None, None]
    points = jnp.sum(jnp.where(hits, rates_all[:, :, None, None, None], 0.0), axis=1)
    own_hits = hits[:, :, reach : reach + slab]
    counts = jnp.sum(own_hits.astype(jnp.float32), axis=1)
    source_ext = rech_ext + points
    observe = gauge[None] + counts

    def rows_of(field, halo):
        return lax.slice_in_dim(field, reach - halo, reach + slab + halo, axis=field.ndim - 3)

    def solve(right_side, halo):
        solution = jnp.zeros_like(right_side)
        residual = right_side
        direction = right_side * first
        for turn in range(CHEB):
            weight = rows_of(perm_ext, halo)
            image = storage * inner(direction) + diffuse(weight, direction)
            solution = inner(solution) + inner(direction)
            residual = inner(residual) - image
            halo -= 1
            direction = (keeps[turn] * inner(direction) + pushes[turn] * residual) * rows_of(
                mask_ext, halo
            )
        return solution + direction, halo

    state, state_halo = solve(source_ext, reach)
    forcing = -diffuse(rows_of(scaled_ext, state_halo)[None], state[:, None])
    forcing = forcing.reshape(tests * cols, slab, rows_y, depth_z)
    forcing_ext = with_halo(forcing, "cell", 1, CHEB)
    change, _ = solve(forcing_ext, CHEB)
    weighted = (
        change.reshape(tests, cols, slab, rows_y, depth_z) * observe[:, None]
    ).reshape(tests * cols, slab, rows_y, depth_z)
    weighted_ext = with_halo(weighted, "cell", 1, CHEB + 1)
    adjoint, _ = solve(weighted_ext, CHEB + 1)
    adjoint = adjoint.reshape(tests, cols, slab + 2, rows_y, depth_z)
    contrib = jnp.sum(pairs(state[:, None], adjoint), axis=0)
    return -0.5 * perm[None] * contrib


def solution(mesh):
    return jax.shard_map(
        shards,
        mesh=mesh,
        in_specs=(
            P("cell", None, None),
            P("test", "cell", None, None),
            P("test", None),
            P("test", None),
            P("test", "cell", None, None),
            P("cell", None, None),
        ),
        out_specs=P("test", "cell", None, None),
        check_vma=False,
    )
```

```python
import math

import jax
import jax.numpy as jnp
from jax import lax
from jax.sharding import PartitionSpec as P

CHEB = 4


storage = 0.02


def with_halo(cells, axis, dim, width):
    count = lax.axis_size(axis)
    ends = count - 1
    head = lax.slice_in_dim(cells, 0, width, axis=dim)
    tail = lax.slice_in_dim(cells, cells.shape[dim] - width, cells.shape[dim], axis=dim)
    return jnp.concatenate(
        [
            lax.ppermute(tail, axis, [(i, i + 1) for i in range(ends)]),
            cells,
            lax.ppermute(head, axis, [(i + 1, i) for i in range(ends)]),
        ],
        axis=dim,
    )


def cheb_table(count):
    highest = storage + 12.0 * math.e
    theta = 0.5 * (highest + storage)
    spread = 0.5 * (highest - storage)
    sigma = theta / spread
    rho = 1.0 / sigma
    keeps = []
    pushes = []
    for turn in range(count):
        after = 1.0 / (2.0 * sigma - rho)
        keeps.append(after * rho)
        pushes.append(2.0 * after / spread)
        rho = after
    return (1.0 / theta, keeps, pushes)


def neighbours(field, back):
    axis = field.ndim - back
    widths = [(0, 0)] * field.ndim
    widths[axis] = (1, 1)
    padded = jnp.pad(field, widths)
    length = field.shape[axis]
    return (
        lax.slice_in_dim(padded, 2, length + 2, axis=axis),
        lax.slice_in_dim(padded, 0, length, axis=axis),
    )


def diffuse(weight_ext, field_ext):
    weight = weight_ext[..., 1:-1, :, :]
    field = field_ext[..., 1:-1, :, :]
    total = 0.5 * (weight + weight_ext[..., 2:, :, :]) * (field - field_ext[..., 2:, :, :])
    total = total + 0.5 * (weight + weight_ext[..., :-2, :, :]) * (
        field - field_ext[..., :-2, :, :]
    )
    for back in (2, 1):
        weight_up, weight_down = neighbours(weight, back)
        field_up, field_down = neighbours(field, back)
        total = (
            total
            + 0.5 * (weight + weight_up) * (field - field_up)
            + 0.5 * (weight + weight_down) * (field - field_down)
        )
    return total


def pairs(left_ext, right_ext):
    left = left_ext[..., 1:-1, :, :]
    right = right_ext[..., 1:-1, :, :]
    total = (left - left_ext[..., 2:, :, :]) * (right - right_ext[..., 2:, :, :])
    total = total + (left - left_ext[..., :-2, :, :]) * (right - right_ext[..., :-2, :, :])
    for back in (2, 1):
        left_up, left_down = neighbours(left, back)
        right_up, right_down = neighbours(right, back)
        total = (
            total
            + (left - left_up) * (right - right_up)
            + (left - left_down) * (right - right_down)
        )
    return total


def inner(field):
    return field[..., 1:-1, :, :]


def shards(log_perm, panel, wells, rates, recharge, gauge):
    place = lax.axis_index("cell")
    parts = lax.axis_size("cell")
    slab, rows_y, depth_z = log_perm.shape
    cols = panel.shape[0]
    tests_here, well_count = wells.shape
    first, keeps, pushes = cheb_table(CHEB)
    reach = 5
    rows_ext = slab + 2 * reach
    perm = jnp.exp(log_perm)
    scaled = perm[None] * panel
    stacked = jnp.concatenate([perm[None], scaled, recharge], axis=0)
    ext = with_halo(stacked, "cell", 1, reach)
    perm_ext = ext[0]
    scaled_ext = ext[1 : 1 + cols]
    rech_own = ext[1 + cols :]
    cells_ext = rows_ext * rows_y * depth_z
    packed = jnp.concatenate(
        [rech_own.reshape(tests_here, cells_ext), wells.astype(jnp.float32), rates], axis=1
    )
    packed = lax.all_gather(packed, "test", axis=0, tiled=True)
    tests = packed.shape[0]
    doubled = jnp.concatenate([packed, packed], axis=0)
    others = lax.dynamic_slice_in_dim(
        doubled, lax.axis_index("test") * tests_here + tests_here, tests - tests_here, axis=0
    )
    rech_others = others[:, :cells_ext].reshape(tests - tests_here, rows_ext, rows_y, depth_z)
    wells_others = others[:, cells_ext : cells_ext + well_count].astype(jnp.int32)
    rates_others = others[:, cells_ext + well_count :]

    gx = place * slab - reach + jnp.arange(rows_ext, dtype=jnp.int32)
    mask_ext = ((gx >= 0) & (gx < parts * slab)).astype(jnp.float32)[:, None, None]
    flat = (
        gx[:, None, None] * (rows_y * depth_z)
        + jnp.arange(rows_y, dtype=jnp.int32)[None, :, None] * depth_z
        + jnp.arange(depth_z, dtype=jnp.int32)[None, None, :]
    )

    def rows_of(field, halo):
        return lax.slice_in_dim(field, reach - halo, reach + slab + halo, axis=field.ndim - 3)

    def solve(right_side, halo):
        solution = jnp.zeros_like(right_side)
        residual = right_side
        direction = right_side * first
        for turn in range(CHEB):
            weight = rows_of(perm_ext, halo)
            image = storage * inner(direction) + diffuse(weight, direction)
            solution = inner(solution) + inner(direction)
            residual = inner(residual) - image
            halo -= 1
            direction = (keeps[turn] * inner(direction) + pushes[turn] * residual) * rows_of(
                mask_ext, halo
            )
        return solution + direction, halo

    def chain(rech_ext, well_rows, rate_rows):
        count = rech_ext.shape[0]
        hits = well_rows[:, :, None, None, None] == flat[None, None]
        points = jnp.sum(jnp.where(hits, rate_rows[:, :, None, None, None], 0.0), axis=1)
        own_hits = hits[:, :, reach : reach + slab]
        counts = jnp.sum(own_hits.astype(jnp.float32), axis=1)
        observe = gauge[None] + counts
        state, state_halo = solve(rech_ext + points, reach)
        forcing = -diffuse(rows_of(scaled_ext, state_halo)[None], state[:, None])
        forcing = forcing.reshape(count * cols, slab, rows_y, depth_z)
        forcing_ext = with_halo(forcing, "cell", 1, CHEB)
        change, _ = solve(forcing_ext, CHEB)
        weighted = (
            change.reshape(count, cols, slab, rows_y, depth_z) * observe[:, None]
        ).reshape(count * cols, slab, rows_y, depth_z)
        weighted_ext = with_halo(weighted, "cell", 1, CHEB + 1)
        adjoint, _ = solve(weighted_ext, CHEB + 1)
        adjoint = adjoint.reshape(count, cols, slab + 2, rows_y, depth_z)
        return jnp.sum(pairs(state[:, None], adjoint), axis=0)

    contrib = chain(rech_own, wells, rates)
    if tests > tests_here:
        contrib = contrib + chain(rech_others, wells_others, rates_others)
    return -0.5 * perm[None] * contrib


def solution(mesh):
    return jax.shard_map(
        shards,
        mesh=mesh,
        in_specs=(
            P("cell", None, None),
            P("test", "cell", None, None),
            P("test", None),
            P("test", None),
            P("test", "cell", None, None),
            P("cell", None, None),
        ),
        out_specs=P("test", "cell", None, None),
        check_vma=False,
    )
```

```python
import math

import jax
import jax.numpy as jnp
from jax import lax
from jax.sharding import PartitionSpec as P

CHEB = 4


storage = 0.02


def with_halo(cells, axis, dim, width):
    count = lax.axis_size(axis)
    ends = count - 1
    head = lax.slice_in_dim(cells, 0, width, axis=dim)
    tail = lax.slice_in_dim(cells, cells.shape[dim] - width, cells.shape[dim], axis=dim)
    return jnp.concatenate(
        [
            lax.ppermute(tail, axis, [(i, i + 1) for i in range(ends)]),
            cells,
            lax.ppermute(head, axis, [(i + 1, i) for i in range(ends)]),
        ],
        axis=dim,
    )


def cheb_table(count):
    highest = storage + 12.0 * math.e
    theta = 0.5 * (highest + storage)
    spread = 0.5 * (highest - storage)
    sigma = theta / spread
    rho = 1.0 / sigma
    keeps = []
    pushes = []
    for turn in range(count):
        after = 1.0 / (2.0 * sigma - rho)
        keeps.append(after * rho)
        pushes.append(2.0 * after / spread)
        rho = after
    return (1.0 / theta, keeps, pushes)


def neighbours(field, back):
    axis = field.ndim - back
    widths = [(0, 0)] * field.ndim
    widths[axis] = (1, 1)
    padded = jnp.pad(field, widths)
    length = field.shape[axis]
    return (
        lax.slice_in_dim(padded, 2, length + 2, axis=axis),
        lax.slice_in_dim(padded, 0, length, axis=axis),
    )


def diffuse(weight_ext, field_ext):
    weight = weight_ext[..., 1:-1, :, :]
    field = field_ext[..., 1:-1, :, :]
    total = 0.5 * (weight + weight_ext[..., 2:, :, :]) * (field - field_ext[..., 2:, :, :])
    total = total + 0.5 * (weight + weight_ext[..., :-2, :, :]) * (
        field - field_ext[..., :-2, :, :]
    )
    for back in (2, 1):
        weight_up, weight_down = neighbours(weight, back)
        field_up, field_down = neighbours(field, back)
        total = (
            total
            + 0.5 * (weight + weight_up) * (field - field_up)
            + 0.5 * (weight + weight_down) * (field - field_down)
        )
    return total


def pairs(left_ext, right_ext):
    left = left_ext[..., 1:-1, :, :]
    right = right_ext[..., 1:-1, :, :]
    total = (left - left_ext[..., 2:, :, :]) * (right - right_ext[..., 2:, :, :])
    total = total + (left - left_ext[..., :-2, :, :]) * (right - right_ext[..., :-2, :, :])
    for back in (2, 1):
        left_up, left_down = neighbours(left, back)
        right_up, right_down = neighbours(right, back)
        total = (
            total
            + (left - left_up) * (right - right_up)
            + (left - left_down) * (right - right_down)
        )
    return total


def inner(field):
    return field[..., 1:-1, :, :]


def shards(log_perm, panel, wells, rates, recharge, gauge):
    place = lax.axis_index("cell")
    parts = lax.axis_size("cell")
    slab, rows_y, depth_z = log_perm.shape
    cols = panel.shape[0]
    tests_here, well_count = wells.shape
    first, keeps, pushes = cheb_table(CHEB)
    reach = 5
    rows_ext = slab + 2 * reach
    perm = jnp.exp(log_perm)
    scaled = perm[None] * panel
    stacked = jnp.concatenate([perm[None], scaled, recharge], axis=0)
    ext = with_halo(stacked, "cell", 1, reach)
    perm_ext = ext[0]
    scaled_ext = ext[1 : 1 + cols]
    rech_own = ext[1 + cols :]
    cells_ext = rows_ext * rows_y * depth_z
    packed = jnp.concatenate(
        [rech_own.reshape(tests_here, cells_ext), wells.astype(jnp.float32), rates], axis=1
    )
    groups = lax.axis_size("test")
    tests = groups * tests_here
    others = jnp.concatenate(
        [
            lax.ppermute(packed, "test", [(i, (i + shift) % groups) for i in range(groups)])
            for shift in range(1, groups)
        ]
        or [packed[:0]],
        axis=0,
    )
    rech_others = others[:, :cells_ext].reshape(tests - tests_here, rows_ext, rows_y, depth_z)
    wells_others = others[:, cells_ext : cells_ext + well_count].astype(jnp.int32)
    rates_others = others[:, cells_ext + well_count :]

    gx = place * slab - reach + jnp.arange(rows_ext, dtype=jnp.int32)
    mask_ext = ((gx >= 0) & (gx < parts * slab)).astype(jnp.float32)[:, None, None]
    flat = (
        gx[:, None, None] * (rows_y * depth_z)
        + jnp.arange(rows_y, dtype=jnp.int32)[None, :, None] * depth_z
        + jnp.arange(depth_z, dtype=jnp.int32)[None, None, :]
    )

    def rows_of(field, halo):
        return lax.slice_in_dim(field, reach - halo, reach + slab + halo, axis=field.ndim - 3)

    def solve(right_side, halo):
        solution = jnp.zeros_like(right_side)
        residual = right_side
        direction = right_side * first
        for turn in range(CHEB):
            weight = rows_of(perm_ext, halo)
            image = storage * inner(direction) + diffuse(weight, direction)
            solution = inner(solution) + inner(direction)
            residual = inner(residual) - image
            halo -= 1
            direction = (keeps[turn] * inner(direction) + pushes[turn] * residual) * rows_of(
                mask_ext, halo
            )
        return solution + direction, halo

    def chain(rech_ext, well_rows, rate_rows):
        count = rech_ext.shape[0]
        hits = well_rows[:, :, None, None, None] == flat[None, None]
        points = jnp.sum(jnp.where(hits, rate_rows[:, :, None, None, None], 0.0), axis=1)
        own_hits = hits[:, :, reach : reach + slab]
        counts = jnp.sum(own_hits.astype(jnp.float32), axis=1)
        observe = gauge[None] + counts
        state, state_halo = solve(rech_ext + points, reach)
        forcing = -diffuse(rows_of(scaled_ext, state_halo)[None], state[:, None])
        forcing = forcing.reshape(count * cols, slab, rows_y, depth_z)
        forcing_ext = with_halo(forcing, "cell", 1, CHEB)
        change, _ = solve(forcing_ext, CHEB)
        weighted = (
            change.reshape(count, cols, slab, rows_y, depth_z) * observe[:, None]
        ).reshape(count * cols, slab, rows_y, depth_z)
        weighted_ext = with_halo(weighted, "cell", 1, CHEB + 1)
        adjoint, _ = solve(weighted_ext, CHEB + 1)
        adjoint = adjoint.reshape(count, cols, slab + 2, rows_y, depth_z)
        return jnp.sum(pairs(state[:, None], adjoint), axis=0)

    contrib = chain(rech_own, wells, rates)
    if tests > tests_here:
        contrib = contrib + chain(rech_others, wells_others, rates_others)
    return -0.5 * perm[None] * contrib


def solution(mesh):
    return jax.shard_map(
        shards,
        mesh=mesh,
        in_specs=(
            P("cell", None, None),
            P("test", "cell", None, None),
            P("test", None),
            P("test", None),
            P("test", "cell", None, None),
            P("cell", None, None),
        ),
        out_specs=P("test", "cell", None, None),
        check_vma=False,
    )
```

```python
import math

import jax
import jax.numpy as jnp
from jax import lax
from jax.sharding import PartitionSpec as P

CHEB = 4


storage = 0.02


def with_halo(cells, axis, dim, width):
    count = lax.axis_size(axis)
    ends = count - 1
    head = lax.slice_in_dim(cells, 0, width, axis=dim)
    tail = lax.slice_in_dim(cells, cells.shape[dim] - width, cells.shape[dim], axis=dim)
    return jnp.concatenate(
        [
            lax.ppermute(tail, axis, [(i, i + 1) for i in range(ends)]),
            cells,
            lax.ppermute(head, axis, [(i + 1, i) for i in range(ends)]),
        ],
        axis=dim,
    )


def cheb_table(count):
    highest = storage + 12.0 * math.e
    theta = 0.5 * (highest + storage)
    spread = 0.5 * (highest - storage)
    sigma = theta / spread
    rho = 1.0 / sigma
    keeps = []
    pushes = []
    for turn in range(count):
        after = 1.0 / (2.0 * sigma - rho)
        keeps.append(after * rho)
        pushes.append(2.0 * after / spread)
        rho = after
    return (1.0 / theta, keeps, pushes)


def neighbours(field, back):
    axis = field.ndim - back
    widths = [(0, 0)] * field.ndim
    widths[axis] = (1, 1)
    padded = jnp.pad(field, widths)
    length = field.shape[axis]
    return (
        lax.slice_in_dim(padded, 2, length + 2, axis=axis),
        lax.slice_in_dim(padded, 0, length, axis=axis),
    )


def diffuse(weight_ext, field_ext):
    weight = weight_ext[..., 1:-1, :, :]
    field = field_ext[..., 1:-1, :, :]
    total = 0.5 * (weight + weight_ext[..., 2:, :, :]) * (field - field_ext[..., 2:, :, :])
    total = total + 0.5 * (weight + weight_ext[..., :-2, :, :]) * (
        field - field_ext[..., :-2, :, :]
    )
    for back in (2, 1):
        weight_up, weight_down = neighbours(weight, back)
        field_up, field_down = neighbours(field, back)
        total = (
            total
            + 0.5 * (weight + weight_up) * (field - field_up)
            + 0.5 * (weight + weight_down) * (field - field_down)
        )
    return total


def pairs(left_ext, right_ext):
    left = left_ext[..., 1:-1, :, :]
    right = right_ext[..., 1:-1, :, :]
    total = (left - left_ext[..., 2:, :, :]) * (right - right_ext[..., 2:, :, :])
    total = total + (left - left_ext[..., :-2, :, :]) * (right - right_ext[..., :-2, :, :])
    for back in (2, 1):
        left_up, left_down = neighbours(left, back)
        right_up, right_down = neighbours(right, back)
        total = (
            total
            + (left - left_up) * (right - right_up)
            + (left - left_down) * (right - right_down)
        )
    return total


def inner(field):
    return field[..., 1:-1, :, :]


def shards(log_perm, panel, wells, rates, recharge, gauge):
    place = lax.axis_index("cell")
    parts = lax.axis_size("cell")
    slab, rows_y, depth_z = log_perm.shape
    cols = panel.shape[0]
    tests_here, well_count = wells.shape
    first, keeps, pushes = cheb_table(CHEB)
    reach = 5
    rows_ext = slab + 2 * reach
    perm = jnp.exp(log_perm)
    scaled = perm[None] * panel
    stacked = jnp.concatenate([perm[None], scaled, recharge], axis=0)
    ext = with_halo(stacked, "cell", 1, reach)
    perm_ext = ext[0]
    scaled_ext = ext[1 : 1 + cols]
    rech_own = ext[1 + cols :]
    cells = slab * rows_y * depth_z
    packed = jnp.concatenate(
        [recharge.reshape(tests_here, cells), wells.astype(jnp.float32), rates], axis=1
    )
    groups = lax.axis_size("test")
    tests = groups * tests_here
    others = jnp.concatenate(
        [
            lax.ppermute(packed, "test", [(i, (i + shift) % groups) for i in range(groups)])
            for shift in range(1, groups)
        ]
        or [packed[:0]],
        axis=0,
    )
    rech_others = with_halo(
        others[:, :cells].reshape(tests - tests_here, slab, rows_y, depth_z), "cell", 1, reach
    )
    wells_others = others[:, cells : cells + well_count].astype(jnp.int32)
    rates_others = others[:, cells + well_count :]

    gx = place * slab - reach + jnp.arange(rows_ext, dtype=jnp.int32)
    mask_ext = ((gx >= 0) & (gx < parts * slab)).astype(jnp.float32)[:, None, None]
    flat = (
        gx[:, None, None] * (rows_y * depth_z)
        + jnp.arange(rows_y, dtype=jnp.int32)[None, :, None] * depth_z
        + jnp.arange(depth_z, dtype=jnp.int32)[None, None, :]
    )

    def rows_of(field, halo):
        return lax.slice_in_dim(field, reach - halo, reach + slab + halo, axis=field.ndim - 3)

    def solve(right_side, halo):
        solution = jnp.zeros_like(right_side)
        residual = right_side
        direction = right_side * first
        for turn in range(CHEB):
            weight = rows_of(perm_ext, halo)
            image = storage * inner(direction) + diffuse(weight, direction)
            solution = inner(solution) + inner(direction)
            residual = inner(residual) - image
            halo -= 1
            direction = (keeps[turn] * inner(direction) + pushes[turn] * residual) * rows_of(
                mask_ext, halo
            )
        return solution + direction, halo

    def chain(rech_ext, well_rows, rate_rows):
        count = rech_ext.shape[0]
        hits = well_rows[:, :, None, None, None] == flat[None, None]
        points = jnp.sum(jnp.where(hits, rate_rows[:, :, None, None, None], 0.0), axis=1)
        own_hits = hits[:, :, reach : reach + slab]
        counts = jnp.sum(own_hits.astype(jnp.float32), axis=1)
        observe = gauge[None] + counts
        state, state_halo = solve(rech_ext + points, reach)
        forcing = -diffuse(rows_of(scaled_ext, state_halo)[None], state[:, None])
        forcing = forcing.reshape(count * cols, slab, rows_y, depth_z)
        forcing_ext = with_halo(forcing, "cell", 1, CHEB)
        change, _ = solve(forcing_ext, CHEB)
        weighted = (
            change.reshape(count, cols, slab, rows_y, depth_z) * observe[:, None]
        ).reshape(count * cols, slab, rows_y, depth_z)
        weighted_ext = with_halo(weighted, "cell", 1, CHEB + 1)
        adjoint, _ = solve(weighted_ext, CHEB + 1)
        adjoint = adjoint.reshape(count, cols, slab + 2, rows_y, depth_z)
        return jnp.sum(pairs(state[:, None], adjoint), axis=0)

    contrib = chain(rech_own, wells, rates)
    if tests > tests_here:
        contrib = contrib + chain(rech_others, wells_others, rates_others)
    return -0.5 * perm[None] * contrib


def solution(mesh):
    return jax.shard_map(
        shards,
        mesh=mesh,
        in_specs=(
            P("cell", None, None),
            P("test", "cell", None, None),
            P("test", None),
            P("test", None),
            P("test", "cell", None, None),
            P("cell", None, None),
        ),
        out_specs=P("test", "cell", None, None),
        check_vma=False,
    )
```

```python
import math

import jax
import jax.numpy as jnp
from jax import lax
from jax.sharding import PartitionSpec as P

CHEB = 4


storage = 0.02


def with_halo(cells, axis, dim, width):
    count = lax.axis_size(axis)
    ends = count - 1
    head = lax.slice_in_dim(cells, 0, width, axis=dim)
    tail = lax.slice_in_dim(cells, cells.shape[dim] - width, cells.shape[dim], axis=dim)
    return jnp.concatenate(
        [
            lax.ppermute(tail, axis, [(i, i + 1) for i in range(ends)]),
            cells,
            lax.ppermute(head, axis, [(i + 1, i) for i in range(ends)]),
        ],
        axis=dim,
    )


def cheb_table(count):
    highest = storage + 12.0 * math.e
    theta = 0.5 * (highest + storage)
    spread = 0.5 * (highest - storage)
    sigma = theta / spread
    rho = 1.0 / sigma
    keeps = []
    pushes = []
    for turn in range(count):
        after = 1.0 / (2.0 * sigma - rho)
        keeps.append(after * rho)
        pushes.append(2.0 * after / spread)
        rho = after
    return (1.0 / theta, keeps, pushes)


def neighbours(field, back):
    axis = field.ndim - back
    widths = [(0, 0)] * field.ndim
    widths[axis] = (1, 1)
    padded = jnp.pad(field, widths)
    length = field.shape[axis]
    return (
        lax.slice_in_dim(padded, 2, length + 2, axis=axis),
        lax.slice_in_dim(padded, 0, length, axis=axis),
    )


def diffuse(weight_ext, field_ext):
    weight = weight_ext[..., 1:-1, :, :]
    field = field_ext[..., 1:-1, :, :]
    total = 0.5 * (weight + weight_ext[..., 2:, :, :]) * (field - field_ext[..., 2:, :, :])
    total = total + 0.5 * (weight + weight_ext[..., :-2, :, :]) * (
        field - field_ext[..., :-2, :, :]
    )
    for back in (2, 1):
        weight_up, weight_down = neighbours(weight, back)
        field_up, field_down = neighbours(field, back)
        total = (
            total
            + 0.5 * (weight + weight_up) * (field - field_up)
            + 0.5 * (weight + weight_down) * (field - field_down)
        )
    return total


def pairs(left_ext, right_ext):
    left = left_ext[..., 1:-1, :, :]
    right = right_ext[..., 1:-1, :, :]
    total = (left - left_ext[..., 2:, :, :]) * (right - right_ext[..., 2:, :, :])
    total = total + (left - left_ext[..., :-2, :, :]) * (right - right_ext[..., :-2, :, :])
    for back in (2, 1):
        left_up, left_down = neighbours(left, back)
        right_up, right_down = neighbours(right, back)
        total = (
            total
            + (left - left_up) * (right - right_up)
            + (left - left_down) * (right - right_down)
        )
    return total


def inner(field):
    return field[..., 1:-1, :, :]


def shards(log_perm, panel, wells, rates, recharge, gauge):
    place = lax.axis_index("cell")
    parts = lax.axis_size("cell")
    slab, rows_y, depth_z = log_perm.shape
    cols = panel.shape[0]
    tests_here, well_count = wells.shape
    first, keeps, pushes = cheb_table(CHEB)
    reach = 5
    rows_ext = slab + 2 * reach
    perm = jnp.exp(log_perm)
    scaled = perm[None] * panel
    stacked = jnp.concatenate([perm[None], scaled, recharge], axis=0)
    ext = with_halo(stacked, "cell", 1, reach)
    perm_ext = ext[0]
    scaled_ext = ext[1 : 1 + cols]
    rech_own = ext[1 + cols :]
    cells = slab * rows_y * depth_z
    packed = jnp.concatenate(
        [recharge.reshape(tests_here, cells), wells.astype(jnp.float32), rates], axis=1
    )
    groups = lax.axis_size("test")
    tests = groups * tests_here
    others = jnp.concatenate(
        [
            lax.ppermute(packed, "test", [(i, (i + shift) % groups) for i in range(groups)])
            for shift in range(1, groups)
        ]
        or [packed[:0]],
        axis=0,
    )
    rech_others = with_halo(
        others[:, :cells].reshape(tests - tests_here, slab, rows_y, depth_z), "cell", 1, reach
    )
    wells_others = others[:, cells : cells + well_count].astype(jnp.int32)
    rates_others = others[:, cells + well_count :]

    gx = place * slab - reach + jnp.arange(rows_ext, dtype=jnp.int32)
    mask_ext = ((gx >= 0) & (gx < parts * slab)).astype(jnp.float32)[:, None, None]
    flat = (
        gx[:, None, None] * (rows_y * depth_z)
        + jnp.arange(rows_y, dtype=jnp.int32)[None, :, None] * depth_z
        + jnp.arange(depth_z, dtype=jnp.int32)[None, None, :]
    )

    def rows_of(field, halo):
        return lax.slice_in_dim(field, reach - halo, reach + slab + halo, axis=field.ndim - 3)

    def solve(right_side, halo):
        solution = jnp.zeros_like(right_side)
        residual = right_side
        direction = right_side * first
        for turn in range(CHEB):
            weight = rows_of(perm_ext, halo)
            image = storage * inner(direction) + diffuse(weight, direction)
            solution = inner(solution) + inner(direction)
            residual = inner(residual) - image
            halo -= 1
            direction = (keeps[turn] * inner(direction) + pushes[turn] * residual) * rows_of(
                mask_ext, halo
            )
        return solution + direction, halo

    def begin(rech_ext, well_rows, rate_rows):
        hits = well_rows[:, :, None, None, None] == flat[None, None]
        points = jnp.sum(jnp.where(hits, rate_rows[:, :, None, None, None], 0.0), axis=1)
        own_hits = hits[:, :, reach : reach + slab]
        counts = jnp.sum(own_hits.astype(jnp.float32), axis=1)
        observe = gauge[None] + counts
        state, state_halo = solve(rech_ext + points, reach)
        forcing = -diffuse(rows_of(scaled_ext, state_halo)[None], state[:, None])
        return state, forcing, observe

    parts_of = [begin(rech_own, wells, rates)]
    if tests > tests_here:
        parts_of.append(begin(rech_others, wells_others, rates_others))
    state, forcing, observe = (jnp.concatenate(group, axis=0) for group in zip(*parts_of))
    forcing = forcing.reshape(tests * cols, slab, rows_y, depth_z)
    forcing_ext = with_halo(forcing, "cell", 1, CHEB)
    change, _ = solve(forcing_ext, CHEB)
    weighted = (
        change.reshape(tests, cols, slab, rows_y, depth_z) * observe[:, None]
    ).reshape(tests * cols, slab, rows_y, depth_z)
    weighted_ext = with_halo(weighted, "cell", 1, CHEB + 1)
    adjoint, _ = solve(weighted_ext, CHEB + 1)
    adjoint = adjoint.reshape(tests, cols, slab + 2, rows_y, depth_z)
    contrib = jnp.sum(pairs(state[:, None], adjoint), axis=0)
    return -0.5 * perm[None] * contrib


def solution(mesh):
    return jax.shard_map(
        shards,
        mesh=mesh,
        in_specs=(
            P("cell", None, None),
            P("test", "cell", None, None),
            P("test", None),
            P("test", None),
            P("test", "cell", None, None),
            P("cell", None, None),
        ),
        out_specs=P("test", "cell", None, None),
        check_vma=False,
    )
```

```python
import math

import jax
import jax.numpy as jnp
from jax import lax
from jax.sharding import PartitionSpec as P

CHEB = 4


storage = 0.02


def with_halo(cells, axis, dim, width):
    count = lax.axis_size(axis)
    ends = count - 1
    head = lax.slice_in_dim(cells, 0, width, axis=dim)
    tail = lax.slice_in_dim(cells, cells.shape[dim] - width, cells.shape[dim], axis=dim)
    return jnp.concatenate(
        [
            lax.ppermute(tail, axis, [(i, i + 1) for i in range(ends)]),
            cells,
            lax.ppermute(head, axis, [(i + 1, i) for i in range(ends)]),
        ],
        axis=dim,
    )


def cheb_table(count):
    highest = storage + 12.0 * math.e
    theta = 0.5 * (highest + storage)
    spread = 0.5 * (highest - storage)
    sigma = theta / spread
    rho = 1.0 / sigma
    keeps = []
    pushes = []
    for turn in range(count):
        after = 1.0 / (2.0 * sigma - rho)
        keeps.append(after * rho)
        pushes.append(2.0 * after / spread)
        rho = after
    return (1.0 / theta, keeps, pushes)


def neighbours(field, back):
    axis = field.ndim - back
    widths = [(0, 0)] * field.ndim
    widths[axis] = (1, 1)
    padded = jnp.pad(field, widths)
    length = field.shape[axis]
    return (
        lax.slice_in_dim(padded, 2, length + 2, axis=axis),
        lax.slice_in_dim(padded, 0, length, axis=axis),
    )


def diffuse(weight_ext, field_ext):
    weight = weight_ext[..., 1:-1, :, :]
    field = field_ext[..., 1:-1, :, :]
    total = 0.5 * (weight + weight_ext[..., 2:, :, :]) * (field - field_ext[..., 2:, :, :])
    total = total + 0.5 * (weight + weight_ext[..., :-2, :, :]) * (
        field - field_ext[..., :-2, :, :]
    )
    for back in (2, 1):
        weight_up, weight_down = neighbours(weight, back)
        field_up, field_down = neighbours(field, back)
        total = (
            total
            + 0.5 * (weight + weight_up) * (field - field_up)
            + 0.5 * (weight + weight_down) * (field - field_down)
        )
    return total


def pairs(left_ext, right_ext):
    left = left_ext[..., 1:-1, :, :]
    right = right_ext[..., 1:-1, :, :]
    total = (left - left_ext[..., 2:, :, :]) * (right - right_ext[..., 2:, :, :])
    total = total + (left - left_ext[..., :-2, :, :]) * (right - right_ext[..., :-2, :, :])
    for back in (2, 1):
        left_up, left_down = neighbours(left, back)
        right_up, right_down = neighbours(right, back)
        total = (
            total
            + (left - left_up) * (right - right_up)
            + (left - left_down) * (right - right_down)
        )
    return total


def inner(field):
    return field[..., 1:-1, :, :]


def shards(log_perm, panel, wells, rates, recharge, gauge):
    place = lax.axis_index("cell")
    parts = lax.axis_size("cell")
    slab, rows_y, depth_z = log_perm.shape
    cols = panel.shape[0]
    tests_here, well_count = wells.shape
    first, keeps, pushes = cheb_table(CHEB)
    reach = 2 * CHEB + 1
    rows_ext = slab + 2 * reach
    perm = jnp.exp(log_perm)
    scaled = perm[None] * panel
    stacked = jnp.concatenate([perm[None], scaled, recharge], axis=0)
    ext = with_halo(stacked, "cell", 1, reach)
    perm_ext = ext[0]
    scaled_ext = ext[1 : 1 + cols]
    rech_own = ext[1 + cols :]
    cells = slab * rows_y * depth_z
    packed = jnp.concatenate(
        [recharge.reshape(tests_here, cells), wells.astype(jnp.float32), rates], axis=1
    )
    groups = lax.axis_size("test")
    tests = groups * tests_here
    others = jnp.concatenate(
        [
            lax.ppermute(packed, "test", [(i, (i + shift) % groups) for i in range(groups)])
            for shift in range(1, groups)
        ]
        or [packed[:0]],
        axis=0,
    )
    rech_others = with_halo(
        others[:, :cells].reshape(tests - tests_here, slab, rows_y, depth_z), "cell", 1, reach
    )
    wells_others = others[:, cells : cells + well_count].astype(jnp.int32)
    rates_others = others[:, cells + well_count :]

    gx = place * slab - reach + jnp.arange(rows_ext, dtype=jnp.int32)
    mask_ext = ((gx >= 0) & (gx < parts * slab)).astype(jnp.float32)[:, None, None]
    flat = (
        gx[:, None, None] * (rows_y * depth_z)
        + jnp.arange(rows_y, dtype=jnp.int32)[None, :, None] * depth_z
        + jnp.arange(depth_z, dtype=jnp.int32)[None, None, :]
    )

    def rows_of(field, halo):
        return lax.slice_in_dim(field, reach - halo, reach + slab + halo, axis=field.ndim - 3)

    def solve(right_side, halo):
        solution = jnp.zeros_like(right_side)
        residual = right_side
        direction = right_side * first
        for turn in range(CHEB):
            weight = rows_of(perm_ext, halo)
            image = storage * inner(direction) + diffuse(weight, direction)
            solution = inner(solution) + inner(direction)
            residual = inner(residual) - image
            halo -= 1
            direction = (keeps[turn] * inner(direction) + pushes[turn] * residual) * rows_of(
                mask_ext, halo
            )
        return solution + direction, halo

    def chain(rech_ext, well_rows, rate_rows):
        count = rech_ext.shape[0]
        hits = well_rows[:, :, None, None, None] == flat[None, None]
        points = jnp.sum(jnp.where(hits, rate_rows[:, :, None, None, None], 0.0), axis=1)
        own_hits = hits[:, :, reach : reach + slab]
        counts = jnp.sum(own_hits.astype(jnp.float32), axis=1)
        observe = gauge[None] + counts
        state, state_halo = solve(rech_ext + points, reach)
        forcing = -diffuse(rows_of(scaled_ext, state_halo)[None], state[:, None])
        forcing = forcing * rows_of(mask_ext, state_halo - 1)
        forcing = forcing.reshape(count * cols, slab + 2 * CHEB, rows_y, depth_z)
        change, _ = solve(forcing, CHEB)
        weighted = (
            change.reshape(count, cols, slab, rows_y, depth_z) * observe[:, None]
        ).reshape(count * cols, slab, rows_y, depth_z)
        weighted_ext = with_halo(weighted, "cell", 1, CHEB + 1)
        adjoint, _ = solve(weighted_ext, CHEB + 1)
        adjoint = adjoint.reshape(count, cols, slab + 2, rows_y, depth_z)
        state = lax.slice_in_dim(state, CHEB, state.shape[1] - CHEB, axis=1)
        return jnp.sum(pairs(state[:, None], adjoint), axis=0)

    contrib = chain(rech_own, wells, rates)
    if tests > tests_here:
        contrib = contrib + chain(rech_others, wells_others, rates_others)
    return -0.5 * perm[None] * contrib


def solution(mesh):
    return jax.shard_map(
        shards,
        mesh=mesh,
        in_specs=(
            P("cell", None, None),
            P("test", "cell", None, None),
            P("test", None),
            P("test", None),
            P("test", "cell", None, None),
            P("cell", None, None),
        ),
        out_specs=P("test", "cell", None, None),
        check_vma=False,
    )
```

```python
import math

import jax
import jax.numpy as jnp
from jax import lax
from jax.sharding import PartitionSpec as P

CHEB = 4


storage = 0.02


def with_halo(cells, axis, dim, width):
    count = lax.axis_size(axis)
    ends = count - 1
    head = lax.slice_in_dim(cells, 0, width, axis=dim)
    tail = lax.slice_in_dim(cells, cells.shape[dim] - width, cells.shape[dim], axis=dim)
    return jnp.concatenate(
        [
            lax.ppermute(tail, axis, [(i, i + 1) for i in range(ends)]),
            cells,
            lax.ppermute(head, axis, [(i + 1, i) for i in range(ends)]),
        ],
        axis=dim,
    )


def cheb_table(count):
    highest = storage + 12.0 * math.e
    theta = 0.5 * (highest + storage)
    spread = 0.5 * (highest - storage)
    sigma = theta / spread
    rho = 1.0 / sigma
    keeps = []
    pushes = []
    for turn in range(count):
        after = 1.0 / (2.0 * sigma - rho)
        keeps.append(after * rho)
        pushes.append(2.0 * after / spread)
        rho = after
    return (1.0 / theta, keeps, pushes)


def neighbours(field, back):
    axis = field.ndim - back
    widths = [(0, 0)] * field.ndim
    widths[axis] = (1, 1)
    padded = jnp.pad(field, widths)
    length = field.shape[axis]
    return (
        lax.slice_in_dim(padded, 2, length + 2, axis=axis),
        lax.slice_in_dim(padded, 0, length, axis=axis),
    )


def diffuse(weight_ext, field_ext):
    weight = weight_ext[..., 1:-1, :, :]
    field = field_ext[..., 1:-1, :, :]
    total = 0.5 * (weight + weight_ext[..., 2:, :, :]) * (field - field_ext[..., 2:, :, :])
    total = total + 0.5 * (weight + weight_ext[..., :-2, :, :]) * (
        field - field_ext[..., :-2, :, :]
    )
    for back in (2, 1):
        weight_up, weight_down = neighbours(weight, back)
        field_up, field_down = neighbours(field, back)
        total = (
            total
            + 0.5 * (weight + weight_up) * (field - field_up)
            + 0.5 * (weight + weight_down) * (field - field_down)
        )
    return total


def faces(weight_ext):
    weight = weight_ext[1:-1]
    weight_up_y, weight_down_y = neighbours(weight, 2)
    weight_up_z, weight_down_z = neighbours(weight, 1)
    return (
        0.5 * (weight + weight_ext[2:]),
        0.5 * (weight + weight_ext[:-2]),
        0.5 * (weight + weight_up_y),
        0.5 * (weight + weight_down_y),
        0.5 * (weight + weight_up_z),
        0.5 * (weight + weight_down_z),
    )


def apply_faces(face, field_ext):
    field = field_ext[..., 1:-1, :, :]
    total = face[0] * (field - field_ext[..., 2:, :, :])
    total = total + face[1] * (field - field_ext[..., :-2, :, :])
    for back, up, down in ((2, face[2], face[3]), (1, face[4], face[5])):
        field_up, field_down = neighbours(field, back)
        total = total + up * (field - field_up) + down * (field - field_down)
    return total


def pairs(left_ext, right_ext):
    left = left_ext[..., 1:-1, :, :]
    right = right_ext[..., 1:-1, :, :]
    total = (left - left_ext[..., 2:, :, :]) * (right - right_ext[..., 2:, :, :])
    total = total + (left - left_ext[..., :-2, :, :]) * (right - right_ext[..., :-2, :, :])
    for back in (2, 1):
        left_up, left_down = neighbours(left, back)
        right_up, right_down = neighbours(right, back)
        total = (
            total
            + (left - left_up) * (right - right_up)
            + (left - left_down) * (right - right_down)
        )
    return total


def inner(field):
    return field[..., 1:-1, :, :]


def shards(log_perm, panel, wells, rates, recharge, gauge):
    place = lax.axis_index("cell")
    parts = lax.axis_size("cell")
    slab, rows_y, depth_z = log_perm.shape
    cols = panel.shape[0]
    tests_here, well_count = wells.shape
    first, keeps, pushes = cheb_table(CHEB)
    reach = 2 * CHEB + 1
    rows_ext = slab + 2 * reach
    perm = jnp.exp(log_perm)
    scaled = perm[None] * panel
    stacked = jnp.concatenate([perm[None], scaled, recharge], axis=0)
    ext = with_halo(stacked, "cell", 1, reach)
    perm_ext = ext[0]
    scaled_ext = ext[1 : 1 + cols]
    rech_own = ext[1 + cols :]
    cells = slab * rows_y * depth_z
    packed = jnp.concatenate(
        [recharge.reshape(tests_here, cells), wells.astype(jnp.float32), rates], axis=1
    )
    groups = lax.axis_size("test")
    tests = groups * tests_here
    others = jnp.concatenate(
        [
            lax.ppermute(packed, "test", [(i, (i + shift) % groups) for i in range(groups)])
            for shift in range(1, groups)
        ]
        or [packed[:0]],
        axis=0,
    )
    rech_others = with_halo(
        others[:, :cells].reshape(tests - tests_here, slab, rows_y, depth_z), "cell", 1, reach
    )
    wells_others = others[:, cells : cells + well_count].astype(jnp.int32)
    rates_others = others[:, cells + well_count :]

    gx = place * slab - reach + jnp.arange(rows_ext, dtype=jnp.int32)
    mask_ext = ((gx >= 0) & (gx < parts * slab)).astype(jnp.float32)[:, None, None]
    flat = (
        gx[:, None, None] * (rows_y * depth_z)
        + jnp.arange(rows_y, dtype=jnp.int32)[None, :, None] * depth_z
        + jnp.arange(depth_z, dtype=jnp.int32)[None, None, :]
    )

    perm_faces = faces(perm_ext)

    def rows_of(field, halo):
        return lax.slice_in_dim(field, reach - halo, reach + slab + halo, axis=field.ndim - 3)

    def solve(right_side, halo):
        solution = jnp.zeros_like(right_side)
        residual = right_side
        direction = right_side * first
        for turn in range(CHEB):
            face = tuple(part[reach - halo : reach + slab + halo - 2] for part in perm_faces)
            image = storage * inner(direction) + apply_faces(face, direction)
            solution = inner(solution) + inner(direction)
            residual = inner(residual) - image
            halo -= 1
            direction = (keeps[turn] * inner(direction) + pushes[turn] * residual) * rows_of(
                mask_ext, halo
            )
        return solution + direction, halo

    def chain(rech_ext, well_rows, rate_rows):
        count = rech_ext.shape[0]
        hits = well_rows[:, :, None, None, None] == flat[None, None]
        points = jnp.sum(jnp.where(hits, rate_rows[:, :, None, None, None], 0.0), axis=1)
        own_hits = hits[:, :, reach : reach + slab]
        counts = jnp.sum(own_hits.astype(jnp.float32), axis=1)
        observe = gauge[None] + counts
        state, state_halo = solve(rech_ext + points, reach)
        forcing = -diffuse(rows_of(scaled_ext, state_halo)[None], state[:, None])
        forcing = forcing * rows_of(mask_ext, state_halo - 1)
        forcing = forcing.reshape(count * cols, slab + 2 * CHEB, rows_y, depth_z)
        change, _ = solve(forcing, CHEB)
        weighted = (
            change.reshape(count, cols, slab, rows_y, depth_z) * observe[:, None]
        ).reshape(count * cols, slab, rows_y, depth_z)
        weighted_ext = with_halo(weighted, "cell", 1, CHEB + 1)
        adjoint, _ = solve(weighted_ext, CHEB + 1)
        adjoint = adjoint.reshape(count, cols, slab + 2, rows_y, depth_z)
        state = lax.slice_in_dim(state, CHEB, state.shape[1] - CHEB, axis=1)
        return jnp.sum(pairs(state[:, None], adjoint), axis=0)

    contrib = chain(rech_own, wells, rates)
    if tests > tests_here:
        contrib = contrib + chain(rech_others, wells_others, rates_others)
    return -0.5 * perm[None] * contrib


def solution(mesh):
    return jax.shard_map(
        shards,
        mesh=mesh,
        in_specs=(
            P("cell", None, None),
            P("test", "cell", None, None),
            P("test", None),
            P("test", None),
            P("test", "cell", None, None),
            P("cell", None, None),
        ),
        out_specs=P("test", "cell", None, None),
        check_vma=False,
    )
```

```python
import functools
import math

import jax
import jax.numpy as jnp
from jax import lax
from jax.experimental import pallas as pl
from jax.experimental.pallas import tpu as pltpu
from jax.sharding import PartitionSpec as P

CHEB = 4


storage = 0.02


def with_halo(cells, axis, dim, width):
    count = lax.axis_size(axis)
    ends = count - 1
    head = lax.slice_in_dim(cells, 0, width, axis=dim)
    tail = lax.slice_in_dim(cells, cells.shape[dim] - width, cells.shape[dim], axis=dim)
    return jnp.concatenate(
        [
            lax.ppermute(tail, axis, [(i, i + 1) for i in range(ends)]),
            cells,
            lax.ppermute(head, axis, [(i + 1, i) for i in range(ends)]),
        ],
        axis=dim,
    )


INTERPRET = False


def solve_kernel(b_ref, k_ref, m_ref, o_ref, sol, res, da, db, *, offset, first, keeps, pushes):
    rows, rows_y, depth_z = sol.shape
    iy = lax.broadcasted_iota(jnp.int32, (rows_y, depth_z), 0)
    iz = lax.broadcasted_iota(jnp.int32, (rows_y, depth_z), 1)

    def init(r, c):
        value = b_ref[0, r]
        res[r] = value
        da[r] = value * first
        sol[r] = jnp.zeros_like(value)
        return c

    lax.fori_loop(0, rows, init, 0)
    bufs = (da, db)
    for turn in range(CHEB):
        src = bufs[turn % 2]
        dst = bufs[(turn + 1) % 2]
        keep = keeps[turn]
        push = pushes[turn]

        def step(r, c, src=src, dst=dst, keep=keep, push=push):
            here = src[r]
            face = r - 1 + offset
            total = k_ref[0, face] * (here - src[r + 1])
            total = total + k_ref[1, face] * (here - src[r - 1])
            up = jnp.where(iy < rows_y - 1, pltpu.roll(here, rows_y - 1, 0), 0.0)
            down = jnp.where(iy > 0, pltpu.roll(here, 1, 0), 0.0)
            total = total + k_ref[2, face] * (here - up) + k_ref[3, face] * (here - down)
            up = jnp.where(iz < depth_z - 1, pltpu.roll(here, depth_z - 1, 1), 0.0)
            down = jnp.where(iz > 0, pltpu.roll(here, 1, 1), 0.0)
            total = total + k_ref[4, face] * (here - up) + k_ref[5, face] * (here - down)
            image = storage * here + total
            sol[r] = sol[r] + here
            fresh = res[r] - image
            res[r] = fresh
            dst[r] = (keep * here + push * fresh) * m_ref[r + offset]
            return c

        lax.fori_loop(turn + 1, rows - 1 - turn, step, 0)
    final = bufs[CHEB % 2]

    def out(r, c):
        o_ref[0, r - CHEB] = sol[r] + final[r]
        return c

    lax.fori_loop(CHEB, rows - CHEB, out, 0)


def kernel_solve(right_side, face_stack, mask_full, offset, first, keeps, pushes):
    fields, rows, rows_y, depth_z = right_side.shape
    body = functools.partial(
        solve_kernel,
        offset=offset,
        first=first,
        keeps=tuple(keeps),
        pushes=tuple(pushes),
    )
    return pl.pallas_call(
        body,
        grid=(fields,),
        in_specs=[
            pl.BlockSpec((1, rows, rows_y, depth_z), lambda f: (f, 0, 0, 0)),
            pl.BlockSpec(face_stack.shape, lambda f: (0, 0, 0, 0)),
            pl.BlockSpec(mask_full.shape, lambda f: (0, 0, 0)),
        ],
        out_specs=pl.BlockSpec((1, rows - 2 * CHEB, rows_y, depth_z), lambda f: (f, 0, 0, 0)),
        out_shape=jax.ShapeDtypeStruct((fields, rows - 2 * CHEB, rows_y, depth_z), jnp.float32),
        scratch_shapes=[pltpu.VMEM((rows, rows_y, depth_z), jnp.float32) for _ in range(4)],
        compiler_params=pltpu.CompilerParams(vmem_limit_bytes=48 * 1024 * 1024),
        interpret=INTERPRET,
    )(right_side, face_stack, mask_full)


def cheb_table(count):
    highest = storage + 12.0 * math.e
    theta = 0.5 * (highest + storage)
    spread = 0.5 * (highest - storage)
    sigma = theta / spread
    rho = 1.0 / sigma
    keeps = []
    pushes = []
    for turn in range(count):
        after = 1.0 / (2.0 * sigma - rho)
        keeps.append(after * rho)
        pushes.append(2.0 * after / spread)
        rho = after
    return (1.0 / theta, keeps, pushes)


def neighbours(field, back):
    axis = field.ndim - back
    widths = [(0, 0)] * field.ndim
    widths[axis] = (1, 1)
    padded = jnp.pad(field, widths)
    length = field.shape[axis]
    return (
        lax.slice_in_dim(padded, 2, length + 2, axis=axis),
        lax.slice_in_dim(padded, 0, length, axis=axis),
    )


def diffuse(weight_ext, field_ext):
    weight = weight_ext[..., 1:-1, :, :]
    field = field_ext[..., 1:-1, :, :]
    total = 0.5 * (weight + weight_ext[..., 2:, :, :]) * (field - field_ext[..., 2:, :, :])
    total = total + 0.5 * (weight + weight_ext[..., :-2, :, :]) * (
        field - field_ext[..., :-2, :, :]
    )
    for back in (2, 1):
        weight_up, weight_down = neighbours(weight, back)
        field_up, field_down = neighbours(field, back)
        total = (
            total
            + 0.5 * (weight + weight_up) * (field - field_up)
            + 0.5 * (weight + weight_down) * (field - field_down)
        )
    return total


def faces(weight_ext):
    weight = weight_ext[1:-1]
    weight_up_y, weight_down_y = neighbours(weight, 2)
    weight_up_z, weight_down_z = neighbours(weight, 1)
    return (
        0.5 * (weight + weight_ext[2:]),
        0.5 * (weight + weight_ext[:-2]),
        0.5 * (weight + weight_up_y),
        0.5 * (weight + weight_down_y),
        0.5 * (weight + weight_up_z),
        0.5 * (weight + weight_down_z),
    )


def apply_faces(face, field_ext):
    field = field_ext[..., 1:-1, :, :]
    total = face[0] * (field - field_ext[..., 2:, :, :])
    total = total + face[1] * (field - field_ext[..., :-2, :, :])
    for back, up, down in ((2, face[2], face[3]), (1, face[4], face[5])):
        field_up, field_down = neighbours(field, back)
        total = total + up * (field - field_up) + down * (field - field_down)
    return total


def pairs(left_ext, right_ext):
    left = left_ext[..., 1:-1, :, :]
    right = right_ext[..., 1:-1, :, :]
    total = (left - left_ext[..., 2:, :, :]) * (right - right_ext[..., 2:, :, :])
    total = total + (left - left_ext[..., :-2, :, :]) * (right - right_ext[..., :-2, :, :])
    for back in (2, 1):
        left_up, left_down = neighbours(left, back)
        right_up, right_down = neighbours(right, back)
        total = (
            total
            + (left - left_up) * (right - right_up)
            + (left - left_down) * (right - right_down)
        )
    return total


def inner(field):
    return field[..., 1:-1, :, :]


def shards(log_perm, panel, wells, rates, recharge, gauge):
    place = lax.axis_index("cell")
    parts = lax.axis_size("cell")
    slab, rows_y, depth_z = log_perm.shape
    cols = panel.shape[0]
    tests_here, well_count = wells.shape
    first, keeps, pushes = cheb_table(CHEB)
    reach = 2 * CHEB + 1
    rows_ext = slab + 2 * reach
    perm = jnp.exp(log_perm)
    scaled = perm[None] * panel
    stacked = jnp.concatenate([perm[None], scaled, recharge], axis=0)
    ext = with_halo(stacked, "cell", 1, reach)
    perm_ext = ext[0]
    scaled_ext = ext[1 : 1 + cols]
    rech_own = ext[1 + cols :]
    cells = slab * rows_y * depth_z
    packed = jnp.concatenate(
        [recharge.reshape(tests_here, cells), wells.astype(jnp.float32), rates], axis=1
    )
    groups = lax.axis_size("test")
    tests = groups * tests_here
    others = jnp.concatenate(
        [
            lax.ppermute(packed, "test", [(i, (i + shift) % groups) for i in range(groups)])
            for shift in range(1, groups)
        ]
        or [packed[:0]],
        axis=0,
    )
    rech_others = with_halo(
        others[:, :cells].reshape(tests - tests_here, slab, rows_y, depth_z), "cell", 1, reach
    )
    wells_others = others[:, cells : cells + well_count].astype(jnp.int32)
    rates_others = others[:, cells + well_count :]

    gx = place * slab - reach + jnp.arange(rows_ext, dtype=jnp.int32)
    mask_ext = ((gx >= 0) & (gx < parts * slab)).astype(jnp.float32)[:, None, None]
    flat = (
        gx[:, None, None] * (rows_y * depth_z)
        + jnp.arange(rows_y, dtype=jnp.int32)[None, :, None] * depth_z
        + jnp.arange(depth_z, dtype=jnp.int32)[None, None, :]
    )

    perm_faces = faces(perm_ext)

    def rows_of(field, halo):
        return lax.slice_in_dim(field, reach - halo, reach + slab + halo, axis=field.ndim - 3)

    face_stack = jnp.stack(perm_faces)
    mask_full = jnp.broadcast_to(mask_ext, (rows_ext, rows_y, depth_z))

    def solve(right_side, halo):
        lead = right_side.shape[:-3]
        flat_side = right_side.reshape((-1,) + right_side.shape[-3:])
        result = kernel_solve(
            flat_side, face_stack, mask_full, reach - halo, first, keeps, pushes
        )
        return result.reshape(lead + result.shape[-3:]), halo - CHEB

    def solve_xla(right_side, halo):
        solution = jnp.zeros_like(right_side)
        residual = right_side
        direction = right_side * first
        for turn in range(CHEB):
            face = tuple(part[reach - halo : reach + slab + halo - 2] for part in perm_faces)
            image = storage * inner(direction) + apply_faces(face, direction)
            solution = inner(solution) + inner(direction)
            residual = inner(residual) - image
            halo -= 1
            direction = (keeps[turn] * inner(direction) + pushes[turn] * residual) * rows_of(
                mask_ext, halo
            )
        return solution + direction, halo

    def chain(rech_ext, well_rows, rate_rows):
        count = rech_ext.shape[0]
        hits = well_rows[:, :, None, None, None] == flat[None, None]
        points = jnp.sum(jnp.where(hits, rate_rows[:, :, None, None, None], 0.0), axis=1)
        own_hits = hits[:, :, reach : reach + slab]
        counts = jnp.sum(own_hits.astype(jnp.float32), axis=1)
        observe = gauge[None] + counts
        state, state_halo = solve(rech_ext + points, reach)
        forcing = -diffuse(rows_of(scaled_ext, state_halo)[None], state[:, None])
        forcing = forcing * rows_of(mask_ext, state_halo - 1)
        forcing = forcing.reshape(count * cols, slab + 2 * CHEB, rows_y, depth_z)
        change, _ = solve(forcing, CHEB)
        weighted = (
            change.reshape(count, cols, slab, rows_y, depth_z) * observe[:, None]
        ).reshape(count * cols, slab, rows_y, depth_z)
        weighted_ext = with_halo(weighted, "cell", 1, CHEB + 1)
        adjoint, _ = solve(weighted_ext, CHEB + 1)
        adjoint = adjoint.reshape(count, cols, slab + 2, rows_y, depth_z)
        state = lax.slice_in_dim(state, CHEB, state.shape[1] - CHEB, axis=1)
        return jnp.sum(pairs(state[:, None], adjoint), axis=0)

    contrib = chain(rech_own, wells, rates)
    if tests > tests_here:
        contrib = contrib + chain(rech_others, wells_others, rates_others)
    return -0.5 * perm[None] * contrib


def solution(mesh):
    return jax.shard_map(
        shards,
        mesh=mesh,
        in_specs=(
            P("cell", None, None),
            P("test", "cell", None, None),
            P("test", None),
            P("test", None),
            P("test", "cell", None, None),
            P("cell", None, None),
        ),
        out_specs=P("test", "cell", None, None),
        check_vma=False,
    )
```

```python
import functools
import math

import jax
import jax.numpy as jnp
from jax import lax
from jax.experimental import pallas as pl
from jax.experimental.pallas import tpu as pltpu
from jax.sharding import PartitionSpec as P

CHEB = 4


storage = 0.02


def with_halo(cells, axis, dim, width):
    count = lax.axis_size(axis)
    ends = count - 1
    head = lax.slice_in_dim(cells, 0, width, axis=dim)
    tail = lax.slice_in_dim(cells, cells.shape[dim] - width, cells.shape[dim], axis=dim)
    return jnp.concatenate(
        [
            lax.ppermute(tail, axis, [(i, i + 1) for i in range(ends)]),
            cells,
            lax.ppermute(head, axis, [(i + 1, i) for i in range(ends)]),
        ],
        axis=dim,
    )


INTERPRET = False


def solve_kernel(b_ref, k_ref, m_ref, o_ref, sol, res, da, db, *, offset, first, keeps, pushes):
    rows, rows_y, depth_z = sol.shape
    iy = lax.broadcasted_iota(jnp.int32, (rows_y, depth_z), 0)
    iz = lax.broadcasted_iota(jnp.int32, (rows_y, depth_z), 1)

    def init(r, c):
        value = b_ref[0, r]
        res[r] = value
        da[r] = value * first
        sol[r] = jnp.zeros_like(value)
        return c

    lax.fori_loop(0, rows, init, 0, unroll=True)
    bufs = (da, db)
    for turn in range(CHEB):
        src = bufs[turn % 2]
        dst = bufs[(turn + 1) % 2]
        keep = keeps[turn]
        push = pushes[turn]

        def step(r, c, src=src, dst=dst, keep=keep, push=push):
            here = src[r]
            face = r - 1 + offset
            total = k_ref[0, face] * (here - src[r + 1])
            total = total + k_ref[1, face] * (here - src[r - 1])
            up = jnp.where(iy < rows_y - 1, pltpu.roll(here, rows_y - 1, 0), 0.0)
            down = jnp.where(iy > 0, pltpu.roll(here, 1, 0), 0.0)
            total = total + k_ref[2, face] * (here - up) + k_ref[3, face] * (here - down)
            up = jnp.where(iz < depth_z - 1, pltpu.roll(here, depth_z - 1, 1), 0.0)
            down = jnp.where(iz > 0, pltpu.roll(here, 1, 1), 0.0)
            total = total + k_ref[4, face] * (here - up) + k_ref[5, face] * (here - down)
            image = storage * here + total
            sol[r] = sol[r] + here
            fresh = res[r] - image
            res[r] = fresh
            dst[r] = (keep * here + push * fresh) * m_ref[r + offset]
            return c

        lax.fori_loop(turn + 1, rows - 1 - turn, step, 0, unroll=True)
    final = bufs[CHEB % 2]

    def out(r, c):
        o_ref[0, r - CHEB] = sol[r] + final[r]
        return c

    lax.fori_loop(CHEB, rows - CHEB, out, 0, unroll=True)


def kernel_solve(right_side, face_stack, mask_full, offset, first, keeps, pushes):
    fields, rows, rows_y, depth_z = right_side.shape
    body = functools.partial(
        solve_kernel,
        offset=offset,
        first=first,
        keeps=tuple(keeps),
        pushes=tuple(pushes),
    )
    return pl.pallas_call(
        body,
        grid=(fields,),
        in_specs=[
            pl.BlockSpec((1, rows, rows_y, depth_z), lambda f: (f, 0, 0, 0)),
            pl.BlockSpec(face_stack.shape, lambda f: (0, 0, 0, 0)),
            pl.BlockSpec(mask_full.shape, lambda f: (0, 0, 0)),
        ],
        out_specs=pl.BlockSpec((1, rows - 2 * CHEB, rows_y, depth_z), lambda f: (f, 0, 0, 0)),
        out_shape=jax.ShapeDtypeStruct((fields, rows - 2 * CHEB, rows_y, depth_z), jnp.float32),
        scratch_shapes=[pltpu.VMEM((rows, rows_y, depth_z), jnp.float32) for _ in range(4)],
        compiler_params=pltpu.CompilerParams(vmem_limit_bytes=48 * 1024 * 1024),
        interpret=INTERPRET,
    )(right_side, face_stack, mask_full)


def cheb_table(count):
    highest = storage + 12.0 * math.e
    theta = 0.5 * (highest + storage)
    spread = 0.5 * (highest - storage)
    sigma = theta / spread
    rho = 1.0 / sigma
    keeps = []
    pushes = []
    for turn in range(count):
        after = 1.0 / (2.0 * sigma - rho)
        keeps.append(after * rho)
        pushes.append(2.0 * after / spread)
        rho = after
    return (1.0 / theta, keeps, pushes)


def neighbours(field, back):
    axis = field.ndim - back
    widths = [(0, 0)] * field.ndim
    widths[axis] = (1, 1)
    padded = jnp.pad(field, widths)
    length = field.shape[axis]
    return (
        lax.slice_in_dim(padded, 2, length + 2, axis=axis),
        lax.slice_in_dim(padded, 0, length, axis=axis),
    )


def diffuse(weight_ext, field_ext):
    weight = weight_ext[..., 1:-1, :, :]
    field = field_ext[..., 1:-1, :, :]
    total = 0.5 * (weight + weight_ext[..., 2:, :, :]) * (field - field_ext[..., 2:, :, :])
    total = total + 0.5 * (weight + weight_ext[..., :-2, :, :]) * (
        field - field_ext[..., :-2, :, :]
    )
    for back in (2, 1):
        weight_up, weight_down = neighbours(weight, back)
        field_up, field_down = neighbours(field, back)
        total = (
            total
            + 0.5 * (weight + weight_up) * (field - field_up)
            + 0.5 * (weight + weight_down) * (field - field_down)
        )
    return total


def faces(weight_ext):
    weight = weight_ext[1:-1]
    weight_up_y, weight_down_y = neighbours(weight, 2)
    weight_up_z, weight_down_z = neighbours(weight, 1)
    return (
        0.5 * (weight + weight_ext[2:]),
        0.5 * (weight + weight_ext[:-2]),
        0.5 * (weight + weight_up_y),
        0.5 * (weight + weight_down_y),
        0.5 * (weight + weight_up_z),
        0.5 * (weight + weight_down_z),
    )


def apply_faces(face, field_ext):
    field = field_ext[..., 1:-1, :, :]
    total = face[0] * (field - field_ext[..., 2:, :, :])
    total = total + face[1] * (field - field_ext[..., :-2, :, :])
    for back, up, down in ((2, face[2], face[3]), (1, face[4], face[5])):
        field_up, field_down = neighbours(field, back)
        total = total + up * (field - field_up) + down * (field - field_down)
    return total


def pairs(left_ext, right_ext):
    left = left_ext[..., 1:-1, :, :]
    right = right_ext[..., 1:-1, :, :]
    total = (left - left_ext[..., 2:, :, :]) * (right - right_ext[..., 2:, :, :])
    total = total + (left - left_ext[..., :-2, :, :]) * (right - right_ext[..., :-2, :, :])
    for back in (2, 1):
        left_up, left_down = neighbours(left, back)
        right_up, right_down = neighbours(right, back)
        total = (
            total
            + (left - left_up) * (right - right_up)
            + (left - left_down) * (right - right_down)
        )
    return total


def inner(field):
    return field[..., 1:-1, :, :]


def shards(log_perm, panel, wells, rates, recharge, gauge):
    place = lax.axis_index("cell")
    parts = lax.axis_size("cell")
    slab, rows_y, depth_z = log_perm.shape
    cols = panel.shape[0]
    tests_here, well_count = wells.shape
    first, keeps, pushes = cheb_table(CHEB)
    reach = 2 * CHEB + 1
    rows_ext = slab + 2 * reach
    perm = jnp.exp(log_perm)
    scaled = perm[None] * panel
    stacked = jnp.concatenate([perm[None], scaled, recharge], axis=0)
    ext = with_halo(stacked, "cell", 1, reach)
    perm_ext = ext[0]
    scaled_ext = ext[1 : 1 + cols]
    rech_own = ext[1 + cols :]
    cells = slab * rows_y * depth_z
    packed = jnp.concatenate(
        [recharge.reshape(tests_here, cells), wells.astype(jnp.float32), rates], axis=1
    )
    groups = lax.axis_size("test")
    tests = groups * tests_here
    others = jnp.concatenate(
        [
            lax.ppermute(packed, "test", [(i, (i + shift) % groups) for i in range(groups)])
            for shift in range(1, groups)
        ]
        or [packed[:0]],
        axis=0,
    )
    rech_others = with_halo(
        others[:, :cells].reshape(tests - tests_here, slab, rows_y, depth_z), "cell", 1, reach
    )
    wells_others = others[:, cells : cells + well_count].astype(jnp.int32)
    rates_others = others[:, cells + well_count :]

    gx = place * slab - reach + jnp.arange(rows_ext, dtype=jnp.int32)
    mask_ext = ((gx >= 0) & (gx < parts * slab)).astype(jnp.float32)[:, None, None]
    flat = (
        gx[:, None, None] * (rows_y * depth_z)
        + jnp.arange(rows_y, dtype=jnp.int32)[None, :, None] * depth_z
        + jnp.arange(depth_z, dtype=jnp.int32)[None, None, :]
    )

    perm_faces = faces(perm_ext)

    def rows_of(field, halo):
        return lax.slice_in_dim(field, reach - halo, reach + slab + halo, axis=field.ndim - 3)

    face_stack = jnp.stack(perm_faces)
    mask_full = jnp.broadcast_to(mask_ext, (rows_ext, rows_y, depth_z))

    def solve(right_side, halo):
        lead = right_side.shape[:-3]
        flat_side = right_side.reshape((-1,) + right_side.shape[-3:])
        result = kernel_solve(
            flat_side, face_stack, mask_full, reach - halo, first, keeps, pushes
        )
        return result.reshape(lead + result.shape[-3:]), halo - CHEB

    def solve_xla(right_side, halo):
        solution = jnp.zeros_like(right_side)
        residual = right_side
        direction = right_side * first
        for turn in range(CHEB):
            face = tuple(part[reach - halo : reach + slab + halo - 2] for part in perm_faces)
            image = storage * inner(direction) + apply_faces(face, direction)
            solution = inner(solution) + inner(direction)
            residual = inner(residual) - image
            halo -= 1
            direction = (keeps[turn] * inner(direction) + pushes[turn] * residual) * rows_of(
                mask_ext, halo
            )
        return solution + direction, halo

    def chain(rech_ext, well_rows, rate_rows):
        count = rech_ext.shape[0]
        hits = well_rows[:, :, None, None, None] == flat[None, None]
        points = jnp.sum(jnp.where(hits, rate_rows[:, :, None, None, None], 0.0), axis=1)
        own_hits = hits[:, :, reach : reach + slab]
        counts = jnp.sum(own_hits.astype(jnp.float32), axis=1)
        observe = gauge[None] + counts
        state, state_halo = solve(rech_ext + points, reach)
        forcing = -diffuse(rows_of(scaled_ext, state_halo)[None], state[:, None])
        forcing = forcing * rows_of(mask_ext, state_halo - 1)
        forcing = forcing.reshape(count * cols, slab + 2 * CHEB, rows_y, depth_z)
        change, _ = solve(forcing, CHEB)
        weighted = (
            change.reshape(count, cols, slab, rows_y, depth_z) * observe[:, None]
        ).reshape(count * cols, slab, rows_y, depth_z)
        weighted_ext = with_halo(weighted, "cell", 1, CHEB + 1)
        adjoint, _ = solve(weighted_ext, CHEB + 1)
        adjoint = adjoint.reshape(count, cols, slab + 2, rows_y, depth_z)
        state = lax.slice_in_dim(state, CHEB, state.shape[1] - CHEB, axis=1)
        return jnp.sum(pairs(state[:, None], adjoint), axis=0)

    contrib = chain(rech_own, wells, rates)
    if tests > tests_here:
        contrib = contrib + chain(rech_others, wells_others, rates_others)
    return -0.5 * perm[None] * contrib


def solution(mesh):
    return jax.shard_map(
        shards,
        mesh=mesh,
        in_specs=(
            P("cell", None, None),
            P("test", "cell", None, None),
            P("test", None),
            P("test", None),
            P("test", "cell", None, None),
            P("cell", None, None),
        ),
        out_specs=P("test", "cell", None, None),
        check_vma=False,
    )
```

```python
import functools
import math

import jax
import jax.numpy as jnp
from jax import lax
from jax.experimental import pallas as pl
from jax.experimental.pallas import tpu as pltpu
from jax.sharding import PartitionSpec as P

CHEB = 4


storage = 0.02


def with_halo(cells, axis, dim, width):
    count = lax.axis_size(axis)
    ends = count - 1
    head = lax.slice_in_dim(cells, 0, width, axis=dim)
    tail = lax.slice_in_dim(cells, cells.shape[dim] - width, cells.shape[dim], axis=dim)
    return jnp.concatenate(
        [
            lax.ppermute(tail, axis, [(i, i + 1) for i in range(ends)]),
            cells,
            lax.ppermute(head, axis, [(i + 1, i) for i in range(ends)]),
        ],
        axis=dim,
    )


INTERPRET = False


def solve_kernel(b_ref, k_ref, m_ref, o_ref, sol, res, da, db, *, offset, first, keeps, pushes):
    rows, rows_y, depth_z = sol.shape
    iy = lax.broadcasted_iota(jnp.int32, (rows_y, depth_z), 0)
    iz = lax.broadcasted_iota(jnp.int32, (rows_y, depth_z), 1)

    def init(r, c):
        value = b_ref[0, r]
        res[r] = value
        da[r] = value * first
        sol[r] = jnp.zeros_like(value)
        return c

    lax.fori_loop(0, rows, init, 0, unroll=True)
    bufs = (da, db)
    for turn in range(CHEB):
        src = bufs[turn % 2]
        dst = bufs[(turn + 1) % 2]
        keep = keeps[turn]
        push = pushes[turn]

        def step(r, c, src=src, dst=dst, keep=keep, push=push):
            here = src[r]
            face = r - 1 + offset
            total = k_ref[0, face] * (here - src[r + 1])
            total = total + k_ref[1, face] * (here - src[r - 1])
            up = jnp.where(iy < rows_y - 1, pltpu.roll(here, rows_y - 1, 0), 0.0)
            down = jnp.where(iy > 0, pltpu.roll(here, 1, 0), 0.0)
            total = total + k_ref[2, face] * (here - up) + k_ref[3, face] * (here - down)
            up = jnp.where(iz < depth_z - 1, pltpu.roll(here, depth_z - 1, 1), 0.0)
            down = jnp.where(iz > 0, pltpu.roll(here, 1, 1), 0.0)
            total = total + k_ref[4, face] * (here - up) + k_ref[5, face] * (here - down)
            image = storage * here + total
            sol[r] = sol[r] + here
            fresh = res[r] - image
            res[r] = fresh
            dst[r] = (keep * here + push * fresh) * m_ref[r + offset]
            return c

        lax.fori_loop(turn + 1, rows - 1 - turn, step, 0, unroll=True)
    final = bufs[CHEB % 2]

    def out(r, c):
        o_ref[0, r - CHEB] = sol[r] + final[r]
        return c

    lax.fori_loop(CHEB, rows - CHEB, out, 0, unroll=True)


def kernel_solve(right_side, face_stack, mask_full, offset, first, keeps, pushes):
    fields, rows, rows_y, depth_z = right_side.shape
    body = functools.partial(
        solve_kernel,
        offset=offset,
        first=first,
        keeps=tuple(keeps),
        pushes=tuple(pushes),
    )
    return pl.pallas_call(
        body,
        grid=(fields,),
        in_specs=[
            pl.BlockSpec((1, rows, rows_y, depth_z), lambda f: (f, 0, 0, 0)),
            pl.BlockSpec(face_stack.shape, lambda f: (0, 0, 0, 0)),
            pl.BlockSpec(mask_full.shape, lambda f: (0, 0, 0)),
        ],
        out_specs=pl.BlockSpec((1, rows - 2 * CHEB, rows_y, depth_z), lambda f: (f, 0, 0, 0)),
        out_shape=jax.ShapeDtypeStruct((fields, rows - 2 * CHEB, rows_y, depth_z), jnp.float32),
        scratch_shapes=[pltpu.VMEM((rows, rows_y, depth_z), jnp.float32) for _ in range(4)],
        compiler_params=pltpu.CompilerParams(vmem_limit_bytes=48 * 1024 * 1024),
        interpret=INTERPRET,
    )(right_side, face_stack, mask_full)


def cheb_table(count):
    highest = storage + 12.0 * math.e
    theta = 0.5 * (highest + storage)
    spread = 0.5 * (highest - storage)
    sigma = theta / spread
    rho = 1.0 / sigma
    keeps = []
    pushes = []
    for turn in range(count):
        after = 1.0 / (2.0 * sigma - rho)
        keeps.append(after * rho)
        pushes.append(2.0 * after / spread)
        rho = after
    return (1.0 / theta, keeps, pushes)


def neighbours(field, back):
    axis = field.ndim - back
    widths = [(0, 0)] * field.ndim
    widths[axis] = (1, 1)
    padded = jnp.pad(field, widths)
    length = field.shape[axis]
    return (
        lax.slice_in_dim(padded, 2, length + 2, axis=axis),
        lax.slice_in_dim(padded, 0, length, axis=axis),
    )


def diffuse(weight_ext, field_ext):
    weight = weight_ext[..., 1:-1, :, :]
    field = field_ext[..., 1:-1, :, :]
    total = 0.5 * (weight + weight_ext[..., 2:, :, :]) * (field - field_ext[..., 2:, :, :])
    total = total + 0.5 * (weight + weight_ext[..., :-2, :, :]) * (
        field - field_ext[..., :-2, :, :]
    )
    for back in (2, 1):
        weight_up, weight_down = neighbours(weight, back)
        field_up, field_down = neighbours(field, back)
        total = (
            total
            + 0.5 * (weight + weight_up) * (field - field_up)
            + 0.5 * (weight + weight_down) * (field - field_down)
        )
    return total


def faces(weight_ext):
    weight = weight_ext[1:-1]
    weight_up_y, weight_down_y = neighbours(weight, 2)
    weight_up_z, weight_down_z = neighbours(weight, 1)
    return (
        0.5 * (weight + weight_ext[2:]),
        0.5 * (weight + weight_ext[:-2]),
        0.5 * (weight + weight_up_y),
        0.5 * (weight + weight_down_y),
        0.5 * (weight + weight_up_z),
        0.5 * (weight + weight_down_z),
    )


def apply_faces(face, field_ext):
    field = field_ext[..., 1:-1, :, :]
    total = face[0] * (field - field_ext[..., 2:, :, :])
    total = total + face[1] * (field - field_ext[..., :-2, :, :])
    for back, up, down in ((2, face[2], face[3]), (1, face[4], face[5])):
        field_up, field_down = neighbours(field, back)
        total = total + up * (field - field_up) + down * (field - field_down)
    return total


def pairs(left_ext, right_ext):
    left = left_ext[..., 1:-1, :, :]
    right = right_ext[..., 1:-1, :, :]
    total = (left - left_ext[..., 2:, :, :]) * (right - right_ext[..., 2:, :, :])
    total = total + (left - left_ext[..., :-2, :, :]) * (right - right_ext[..., :-2, :, :])
    for back in (2, 1):
        left_up, left_down = neighbours(left, back)
        right_up, right_down = neighbours(right, back)
        total = (
            total
            + (left - left_up) * (right - right_up)
            + (left - left_down) * (right - right_down)
        )
    return total


def inner(field):
    return field[..., 1:-1, :, :]


def shards(log_perm, panel, wells, rates, recharge, gauge):
    place = lax.axis_index("cell")
    parts = lax.axis_size("cell")
    slab, rows_y, depth_z = log_perm.shape
    cols = panel.shape[0]
    tests_here, well_count = wells.shape
    first, keeps, pushes = cheb_table(CHEB)
    reach = 2 * CHEB + 1
    rows_ext = slab + 2 * reach
    perm = jnp.exp(log_perm)
    scaled = perm[None] * panel
    stacked = jnp.concatenate([perm[None], scaled, recharge], axis=0)
    ext = with_halo(stacked, "cell", 1, reach)
    perm_ext = ext[0]
    scaled_ext = ext[1 : 1 + cols]
    rech_own = ext[1 + cols :]
    cells = slab * rows_y * depth_z
    packed = jnp.concatenate(
        [recharge.reshape(tests_here, cells), wells.astype(jnp.float32), rates], axis=1
    )
    groups = lax.axis_size("test")
    tests = groups * tests_here
    others = jnp.concatenate(
        [
            lax.ppermute(packed, "test", [(i, (i + shift) % groups) for i in range(groups)])
            for shift in range(1, groups)
        ]
        or [packed[:0]],
        axis=0,
    )
    rech_others = with_halo(
        others[:, :cells].reshape(tests - tests_here, slab, rows_y, depth_z), "cell", 1, reach
    )
    wells_others = others[:, cells : cells + well_count].astype(jnp.int32)
    rates_others = others[:, cells + well_count :]

    gx = place * slab - reach + jnp.arange(rows_ext, dtype=jnp.int32)
    mask_ext = ((gx >= 0) & (gx < parts * slab)).astype(jnp.float32)[:, None, None]
    flat = (
        gx[:, None, None] * (rows_y * depth_z)
        + jnp.arange(rows_y, dtype=jnp.int32)[None, :, None] * depth_z
        + jnp.arange(depth_z, dtype=jnp.int32)[None, None, :]
    )

    perm_faces = faces(perm_ext)

    def rows_of(field, halo):
        return lax.slice_in_dim(field, reach - halo, reach + slab + halo, axis=field.ndim - 3)

    face_stack = jnp.stack(perm_faces)
    mask_full = jnp.broadcast_to(mask_ext, (rows_ext, rows_y, depth_z))

    def solve(right_side, halo):
        lead = right_side.shape[:-3]
        flat_side = right_side.reshape((-1,) + right_side.shape[-3:])
        result = kernel_solve(
            flat_side, face_stack, mask_full, reach - halo, first, keeps, pushes
        )
        return result.reshape(lead + result.shape[-3:]), halo - CHEB

    def solve_xla(right_side, halo):
        solution = jnp.zeros_like(right_side)
        residual = right_side
        direction = right_side * first
        for turn in range(CHEB):
            face = tuple(part[reach - halo : reach + slab + halo - 2] for part in perm_faces)
            image = storage * inner(direction) + apply_faces(face, direction)
            solution = inner(solution) + inner(direction)
            residual = inner(residual) - image
            halo -= 1
            direction = (keeps[turn] * inner(direction) + pushes[turn] * residual) * rows_of(
                mask_ext, halo
            )
        return solution + direction, halo

    def begin(rech_ext, well_rows, rate_rows):
        hits = well_rows[:, :, None, None, None] == flat[None, None]
        points = jnp.sum(jnp.where(hits, rate_rows[:, :, None, None, None], 0.0), axis=1)
        own_hits = hits[:, :, reach : reach + slab]
        counts = jnp.sum(own_hits.astype(jnp.float32), axis=1)
        observe = gauge[None] + counts
        state, state_halo = solve(rech_ext + points, reach)
        forcing = -diffuse(rows_of(scaled_ext, state_halo)[None], state[:, None])
        forcing = forcing * rows_of(mask_ext, state_halo - 1)
        state = lax.slice_in_dim(state, CHEB, state.shape[1] - CHEB, axis=1)
        return state, forcing, observe

    parts_of = [begin(rech_own, wells, rates)]
    if tests > tests_here:
        parts_of.append(begin(rech_others, wells_others, rates_others))
    state, forcing, observe = (jnp.concatenate(group, axis=0) for group in zip(*parts_of))
    forcing = forcing.reshape(tests * cols, slab + 2 * CHEB, rows_y, depth_z)
    change, _ = solve(forcing, CHEB)
    weighted = (
        change.reshape(tests, cols, slab, rows_y, depth_z) * observe[:, None]
    ).reshape(tests * cols, slab, rows_y, depth_z)
    weighted_ext = with_halo(weighted, "cell", 1, CHEB + 1)
    adjoint, _ = solve(weighted_ext, CHEB + 1)
    adjoint = adjoint.reshape(tests, cols, slab + 2, rows_y, depth_z)
    contrib = jnp.sum(pairs(state[:, None], adjoint), axis=0)
    return -0.5 * perm[None] * contrib


def solution(mesh):
    return jax.shard_map(
        shards,
        mesh=mesh,
        in_specs=(
            P("cell", None, None),
            P("test", "cell", None, None),
            P("test", None),
            P("test", None),
            P("test", "cell", None, None),
            P("cell", None, None),
        ),
        out_specs=P("test", "cell", None, None),
        check_vma=False,
    )
```

```python
import functools
import math

import jax
import jax.numpy as jnp
from jax import lax
from jax.experimental import pallas as pl
from jax.experimental.pallas import tpu as pltpu
from jax.sharding import PartitionSpec as P

CHEB = 4


storage = 0.02


def with_halo(cells, axis, dim, width):
    count = lax.axis_size(axis)
    ends = count - 1
    head = lax.slice_in_dim(cells, 0, width, axis=dim)
    tail = lax.slice_in_dim(cells, cells.shape[dim] - width, cells.shape[dim], axis=dim)
    return jnp.concatenate(
        [
            lax.ppermute(tail, axis, [(i, i + 1) for i in range(ends)]),
            cells,
            lax.ppermute(head, axis, [(i + 1, i) for i in range(ends)]),
        ],
        axis=dim,
    )


INTERPRET = False


def solve_kernel(b_ref, k_ref, m_ref, o_ref, sol, res, da, db, *, offset, first, keeps, pushes):
    rows, rows_y, depth_z = sol.shape
    iy = lax.broadcasted_iota(jnp.int32, (rows_y, depth_z), 0)
    iz = lax.broadcasted_iota(jnp.int32, (rows_y, depth_z), 1)

    def init(r, c):
        da[r] = b_ref[0, r] * first
        return c

    lax.fori_loop(0, rows, init, 0, unroll=True)
    bufs = (da, db)
    for turn in range(CHEB):
        src = bufs[turn % 2]
        dst = bufs[(turn + 1) % 2]
        keep = keeps[turn]
        push = pushes[turn]

        def step(r, c, turn=turn, src=src, dst=dst, keep=keep, push=push):
            here = src[r]
            face = r - 1 + offset
            total = k_ref[0, face] * (here - src[r + 1])
            total = total + k_ref[1, face] * (here - src[r - 1])
            up = jnp.where(iy < rows_y - 1, pltpu.roll(here, rows_y - 1, 0), 0.0)
            down = jnp.where(iy > 0, pltpu.roll(here, 1, 0), 0.0)
            total = total + k_ref[2, face] * (here - up) + k_ref[3, face] * (here - down)
            up = jnp.where(iz < depth_z - 1, pltpu.roll(here, depth_z - 1, 1), 0.0)
            down = jnp.where(iz > 0, pltpu.roll(here, 1, 1), 0.0)
            total = total + k_ref[4, face] * (here - up) + k_ref[5, face] * (here - down)
            image = storage * here + total
            if turn == 0:
                summed = here
                fresh = b_ref[0, r] - image
            else:
                summed = sol[r] + here
                fresh = res[r] - image
            after = (keep * here + push * fresh) * m_ref[r + offset]
            if turn == CHEB - 1:
                o_ref[0, r - CHEB] = summed + after
            else:
                sol[r] = summed
                res[r] = fresh
                dst[r] = after
            return c

        lax.fori_loop(turn + 1, rows - 1 - turn, step, 0, unroll=True)


def kernel_solve(right_side, face_stack, mask_full, offset, first, keeps, pushes):
    fields, rows, rows_y, depth_z = right_side.shape
    body = functools.partial(
        solve_kernel,
        offset=offset,
        first=first,
        keeps=tuple(keeps),
        pushes=tuple(pushes),
    )
    return pl.pallas_call(
        body,
        grid=(fields,),
        in_specs=[
            pl.BlockSpec((1, rows, rows_y, depth_z), lambda f: (f, 0, 0, 0)),
            pl.BlockSpec(face_stack.shape, lambda f: (0, 0, 0, 0)),
            pl.BlockSpec(mask_full.shape, lambda f: (0, 0, 0)),
        ],
        out_specs=pl.BlockSpec((1, rows - 2 * CHEB, rows_y, depth_z), lambda f: (f, 0, 0, 0)),
        out_shape=jax.ShapeDtypeStruct((fields, rows - 2 * CHEB, rows_y, depth_z), jnp.float32),
        scratch_shapes=[pltpu.VMEM((rows, rows_y, depth_z), jnp.float32) for _ in range(4)],
        compiler_params=pltpu.CompilerParams(vmem_limit_bytes=48 * 1024 * 1024),
        interpret=INTERPRET,
    )(right_side, face_stack, mask_full)


def cheb_table(count):
    highest = storage + 12.0 * math.e
    theta = 0.5 * (highest + storage)
    spread = 0.5 * (highest - storage)
    sigma = theta / spread
    rho = 1.0 / sigma
    keeps = []
    pushes = []
    for turn in range(count):
        after = 1.0 / (2.0 * sigma - rho)
        keeps.append(after * rho)
        pushes.append(2.0 * after / spread)
        rho = after
    return (1.0 / theta, keeps, pushes)


def neighbours(field, back):
    axis = field.ndim - back
    widths = [(0, 0)] * field.ndim
    widths[axis] = (1, 1)
    padded = jnp.pad(field, widths)
    length = field.shape[axis]
    return (
        lax.slice_in_dim(padded, 2, length + 2, axis=axis),
        lax.slice_in_dim(padded, 0, length, axis=axis),
    )


def diffuse(weight_ext, field_ext):
    weight = weight_ext[..., 1:-1, :, :]
    field = field_ext[..., 1:-1, :, :]
    total = 0.5 * (weight + weight_ext[..., 2:, :, :]) * (field - field_ext[..., 2:, :, :])
    total = total + 0.5 * (weight + weight_ext[..., :-2, :, :]) * (
        field - field_ext[..., :-2, :, :]
    )
    for back in (2, 1):
        weight_up, weight_down = neighbours(weight, back)
        field_up, field_down = neighbours(field, back)
        total = (
            total
            + 0.5 * (weight + weight_up) * (field - field_up)
            + 0.5 * (weight + weight_down) * (field - field_down)
        )
    return total


def faces(weight_ext):
    weight = weight_ext[1:-1]
    weight_up_y, weight_down_y = neighbours(weight, 2)
    weight_up_z, weight_down_z = neighbours(weight, 1)
    return (
        0.5 * (weight + weight_ext[2:]),
        0.5 * (weight + weight_ext[:-2]),
        0.5 * (weight + weight_up_y),
        0.5 * (weight + weight_down_y),
        0.5 * (weight + weight_up_z),
        0.5 * (weight + weight_down_z),
    )


def apply_faces(face, field_ext):
    field = field_ext[..., 1:-1, :, :]
    total = face[0] * (field - field_ext[..., 2:, :, :])
    total = total + face[1] * (field - field_ext[..., :-2, :, :])
    for back, up, down in ((2, face[2], face[3]), (1, face[4], face[5])):
        field_up, field_down = neighbours(field, back)
        total = total + up * (field - field_up) + down * (field - field_down)
    return total


def pairs(left_ext, right_ext):
    left = left_ext[..., 1:-1, :, :]
    right = right_ext[..., 1:-1, :, :]
    total = (left - left_ext[..., 2:, :, :]) * (right - right_ext[..., 2:, :, :])
    total = total + (left - left_ext[..., :-2, :, :]) * (right - right_ext[..., :-2, :, :])
    for back in (2, 1):
        left_up, left_down = neighbours(left, back)
        right_up, right_down = neighbours(right, back)
        total = (
            total
            + (left - left_up) * (right - right_up)
            + (left - left_down) * (right - right_down)
        )
    return total


def inner(field):
    return field[..., 1:-1, :, :]


def shards(log_perm, panel, wells, rates, recharge, gauge):
    place = lax.axis_index("cell")
    parts = lax.axis_size("cell")
    slab, rows_y, depth_z = log_perm.shape
    cols = panel.shape[0]
    tests_here, well_count = wells.shape
    first, keeps, pushes = cheb_table(CHEB)
    reach = 2 * CHEB + 1
    rows_ext = slab + 2 * reach
    perm = jnp.exp(log_perm)
    scaled = perm[None] * panel
    stacked = jnp.concatenate([perm[None], scaled, recharge], axis=0)
    ext = with_halo(stacked, "cell", 1, reach)
    perm_ext = ext[0]
    scaled_ext = ext[1 : 1 + cols]
    rech_own = ext[1 + cols :]
    cells = slab * rows_y * depth_z
    packed = jnp.concatenate(
        [recharge.reshape(tests_here, cells), wells.astype(jnp.float32), rates], axis=1
    )
    groups = lax.axis_size("test")
    tests = groups * tests_here
    others = jnp.concatenate(
        [
            lax.ppermute(packed, "test", [(i, (i + shift) % groups) for i in range(groups)])
            for shift in range(1, groups)
        ]
        or [packed[:0]],
        axis=0,
    )
    rech_others = with_halo(
        others[:, :cells].reshape(tests - tests_here, slab, rows_y, depth_z), "cell", 1, reach
    )
    wells_others = others[:, cells : cells + well_count].astype(jnp.int32)
    rates_others = others[:, cells + well_count :]

    gx = place * slab - reach + jnp.arange(rows_ext, dtype=jnp.int32)
    mask_ext = ((gx >= 0) & (gx < parts * slab)).astype(jnp.float32)[:, None, None]
    flat = (
        gx[:, None, None] * (rows_y * depth_z)
        + jnp.arange(rows_y, dtype=jnp.int32)[None, :, None] * depth_z
        + jnp.arange(depth_z, dtype=jnp.int32)[None, None, :]
    )

    perm_faces = faces(perm_ext)

    def rows_of(field, halo):
        return lax.slice_in_dim(field, reach - halo, reach + slab + halo, axis=field.ndim - 3)

    face_stack = jnp.stack(perm_faces)
    mask_full = jnp.broadcast_to(mask_ext, (rows_ext, rows_y, depth_z))

    def solve(right_side, halo):
        lead = right_side.shape[:-3]
        flat_side = right_side.reshape((-1,) + right_side.shape[-3:])
        result = kernel_solve(
            flat_side, face_stack, mask_full, reach - halo, first, keeps, pushes
        )
        return result.reshape(lead + result.shape[-3:]), halo - CHEB

    def solve_xla(right_side, halo):
        solution = jnp.zeros_like(right_side)
        residual = right_side
        direction = right_side * first
        for turn in range(CHEB):
            face = tuple(part[reach - halo : reach + slab + halo - 2] for part in perm_faces)
            image = storage * inner(direction) + apply_faces(face, direction)
            solution = inner(solution) + inner(direction)
            residual = inner(residual) - image
            halo -= 1
            direction = (keeps[turn] * inner(direction) + pushes[turn] * residual) * rows_of(
                mask_ext, halo
            )
        return solution + direction, halo

    def begin(rech_ext, well_rows, rate_rows):
        hits = well_rows[:, :, None, None, None] == flat[None, None]
        points = jnp.sum(jnp.where(hits, rate_rows[:, :, None, None, None], 0.0), axis=1)
        own_hits = hits[:, :, reach : reach + slab]
        counts = jnp.sum(own_hits.astype(jnp.float32), axis=1)
        observe = gauge[None] + counts
        state, state_halo = solve(rech_ext + points, reach)
        forcing = -diffuse(rows_of(scaled_ext, state_halo)[None], state[:, None])
        forcing = forcing * rows_of(mask_ext, state_halo - 1)
        state = lax.slice_in_dim(state, CHEB, state.shape[1] - CHEB, axis=1)
        return state, forcing, observe

    parts_of = [begin(rech_own, wells, rates)]
    if tests > tests_here:
        parts_of.append(begin(rech_others, wells_others, rates_others))
    state, forcing, observe = (jnp.concatenate(group, axis=0) for group in zip(*parts_of))
    forcing = forcing.reshape(tests * cols, slab + 2 * CHEB, rows_y, depth_z)
    change, _ = solve(forcing, CHEB)
    weighted = (
        change.reshape(tests, cols, slab, rows_y, depth_z) * observe[:, None]
    ).reshape(tests * cols, slab, rows_y, depth_z)
    weighted_ext = with_halo(weighted, "cell", 1, CHEB + 1)
    adjoint, _ = solve(weighted_ext, CHEB + 1)
    adjoint = adjoint.reshape(tests, cols, slab + 2, rows_y, depth_z)
    contrib = jnp.sum(pairs(state[:, None], adjoint), axis=0)
    return -0.5 * perm[None] * contrib


def solution(mesh):
    return jax.shard_map(
        shards,
        mesh=mesh,
        in_specs=(
            P("cell", None, None),
            P("test", "cell", None, None),
            P("test", None),
            P("test", None),
            P("test", "cell", None, None),
            P("cell", None, None),
        ),
        out_specs=P("test", "cell", None, None),
        check_vma=False,
    )
```

```python
import functools
import math

import jax
import jax.numpy as jnp
from jax import lax
from jax.experimental import pallas as pl
from jax.experimental.pallas import tpu as pltpu
from jax.sharding import PartitionSpec as P

CHEB = 4


storage = 0.02


def with_halo(cells, axis, dim, width):
    count = lax.axis_size(axis)
    ends = count - 1
    head = lax.slice_in_dim(cells, 0, width, axis=dim)
    tail = lax.slice_in_dim(cells, cells.shape[dim] - width, cells.shape[dim], axis=dim)
    return jnp.concatenate(
        [
            lax.ppermute(tail, axis, [(i, i + 1) for i in range(ends)]),
            cells,
            lax.ppermute(head, axis, [(i + 1, i) for i in range(ends)]),
        ],
        axis=dim,
    )


INTERPRET = False


def solve_kernel(b_ref, k_ref, m_ref, o_ref, sol, res, da, db, *, offset, first, keeps, pushes):
    rows, rows_y, depth_z = sol.shape

    def init(r, c):
        da[r] = b_ref[0, r] * first
        return c

    lax.fori_loop(0, rows, init, 0, unroll=True)
    bufs = (da, db)
    for turn in range(CHEB):
        src = bufs[turn % 2]
        dst = bufs[(turn + 1) % 2]
        keep = keeps[turn]
        push = pushes[turn]

        def step(r, c, turn=turn, src=src, dst=dst, keep=keep, push=push):
            here = src[r]
            face = r - 1 + offset
            image = k_ref[6, face] * here - k_ref[0, face] * src[r + 1]
            image = image - k_ref[1, face] * src[r - 1]
            image = image - k_ref[2, face] * pltpu.roll(here, rows_y - 1, 0)
            image = image - k_ref[3, face] * pltpu.roll(here, 1, 0)
            image = image - k_ref[4, face] * pltpu.roll(here, depth_z - 1, 1)
            image = image - k_ref[5, face] * pltpu.roll(here, 1, 1)
            if turn == 0:
                summed = here
                fresh = b_ref[0, r] - image
            else:
                summed = sol[r] + here
                fresh = res[r] - image
            after = (keep * here + push * fresh) * m_ref[r + offset]
            if turn == CHEB - 1:
                o_ref[0, r - CHEB] = summed + after
            else:
                sol[r] = summed
                res[r] = fresh
                dst[r] = after
            return c

        lax.fori_loop(turn + 1, rows - 1 - turn, step, 0, unroll=True)


def kernel_solve(right_side, face_stack, mask_full, offset, first, keeps, pushes):
    fields, rows, rows_y, depth_z = right_side.shape
    body = functools.partial(
        solve_kernel,
        offset=offset,
        first=first,
        keeps=tuple(keeps),
        pushes=tuple(pushes),
    )
    return pl.pallas_call(
        body,
        grid=(fields,),
        in_specs=[
            pl.BlockSpec((1, rows, rows_y, depth_z), lambda f: (f, 0, 0, 0)),
            pl.BlockSpec(face_stack.shape, lambda f: (0, 0, 0, 0)),
            pl.BlockSpec(mask_full.shape, lambda f: (0, 0, 0)),
        ],
        out_specs=pl.BlockSpec((1, rows - 2 * CHEB, rows_y, depth_z), lambda f: (f, 0, 0, 0)),
        out_shape=jax.ShapeDtypeStruct((fields, rows - 2 * CHEB, rows_y, depth_z), jnp.float32),
        scratch_shapes=[pltpu.VMEM((rows, rows_y, depth_z), jnp.float32) for _ in range(4)],
        compiler_params=pltpu.CompilerParams(vmem_limit_bytes=48 * 1024 * 1024),
        interpret=INTERPRET,
    )(right_side, face_stack, mask_full)


def cheb_table(count):
    highest = storage + 12.0 * math.e
    theta = 0.5 * (highest + storage)
    spread = 0.5 * (highest - storage)
    sigma = theta / spread
    rho = 1.0 / sigma
    keeps = []
    pushes = []
    for turn in range(count):
        after = 1.0 / (2.0 * sigma - rho)
        keeps.append(after * rho)
        pushes.append(2.0 * after / spread)
        rho = after
    return (1.0 / theta, keeps, pushes)


def neighbours(field, back):
    axis = field.ndim - back
    widths = [(0, 0)] * field.ndim
    widths[axis] = (1, 1)
    padded = jnp.pad(field, widths)
    length = field.shape[axis]
    return (
        lax.slice_in_dim(padded, 2, length + 2, axis=axis),
        lax.slice_in_dim(padded, 0, length, axis=axis),
    )


def diffuse(weight_ext, field_ext):
    weight = weight_ext[..., 1:-1, :, :]
    field = field_ext[..., 1:-1, :, :]
    total = 0.5 * (weight + weight_ext[..., 2:, :, :]) * (field - field_ext[..., 2:, :, :])
    total = total + 0.5 * (weight + weight_ext[..., :-2, :, :]) * (
        field - field_ext[..., :-2, :, :]
    )
    for back in (2, 1):
        weight_up, weight_down = neighbours(weight, back)
        field_up, field_down = neighbours(field, back)
        total = (
            total
            + 0.5 * (weight + weight_up) * (field - field_up)
            + 0.5 * (weight + weight_down) * (field - field_down)
        )
    return total


def faces(weight_ext):
    weight = weight_ext[1:-1]
    weight_up_y, weight_down_y = neighbours(weight, 2)
    weight_up_z, weight_down_z = neighbours(weight, 1)
    return (
        0.5 * (weight + weight_ext[2:]),
        0.5 * (weight + weight_ext[:-2]),
        0.5 * (weight + weight_up_y),
        0.5 * (weight + weight_down_y),
        0.5 * (weight + weight_up_z),
        0.5 * (weight + weight_down_z),
    )


def apply_faces(face, field_ext):
    field = field_ext[..., 1:-1, :, :]
    total = face[0] * (field - field_ext[..., 2:, :, :])
    total = total + face[1] * (field - field_ext[..., :-2, :, :])
    for back, up, down in ((2, face[2], face[3]), (1, face[4], face[5])):
        field_up, field_down = neighbours(field, back)
        total = total + up * (field - field_up) + down * (field - field_down)
    return total


def pairs(left_ext, right_ext):
    left = left_ext[..., 1:-1, :, :]
    right = right_ext[..., 1:-1, :, :]
    total = (left - left_ext[..., 2:, :, :]) * (right - right_ext[..., 2:, :, :])
    total = total + (left - left_ext[..., :-2, :, :]) * (right - right_ext[..., :-2, :, :])
    for back in (2, 1):
        left_up, left_down = neighbours(left, back)
        right_up, right_down = neighbours(right, back)
        total = (
            total
            + (left - left_up) * (right - right_up)
            + (left - left_down) * (right - right_down)
        )
    return total


def inner(field):
    return field[..., 1:-1, :, :]


def shards(log_perm, panel, wells, rates, recharge, gauge):
    place = lax.axis_index("cell")
    parts = lax.axis_size("cell")
    slab, rows_y, depth_z = log_perm.shape
    cols = panel.shape[0]
    tests_here, well_count = wells.shape
    first, keeps, pushes = cheb_table(CHEB)
    reach = 2 * CHEB + 1
    rows_ext = slab + 2 * reach
    perm = jnp.exp(log_perm)
    scaled = perm[None] * panel
    stacked = jnp.concatenate([perm[None], scaled, recharge], axis=0)
    ext = with_halo(stacked, "cell", 1, reach)
    perm_ext = ext[0]
    scaled_ext = ext[1 : 1 + cols]
    rech_own = ext[1 + cols :]
    cells = slab * rows_y * depth_z
    packed = jnp.concatenate(
        [recharge.reshape(tests_here, cells), wells.astype(jnp.float32), rates], axis=1
    )
    groups = lax.axis_size("test")
    tests = groups * tests_here
    others = jnp.concatenate(
        [
            lax.ppermute(packed, "test", [(i, (i + shift) % groups) for i in range(groups)])
            for shift in range(1, groups)
        ]
        or [packed[:0]],
        axis=0,
    )
    rech_others = with_halo(
        others[:, :cells].reshape(tests - tests_here, slab, rows_y, depth_z), "cell", 1, reach
    )
    wells_others = others[:, cells : cells + well_count].astype(jnp.int32)
    rates_others = others[:, cells + well_count :]

    gx = place * slab - reach + jnp.arange(rows_ext, dtype=jnp.int32)
    mask_ext = ((gx >= 0) & (gx < parts * slab)).astype(jnp.float32)[:, None, None]
    flat = (
        gx[:, None, None] * (rows_y * depth_z)
        + jnp.arange(rows_y, dtype=jnp.int32)[None, :, None] * depth_z
        + jnp.arange(depth_z, dtype=jnp.int32)[None, None, :]
    )

    perm_faces = faces(perm_ext)

    def rows_of(field, halo):
        return lax.slice_in_dim(field, reach - halo, reach + slab + halo, axis=field.ndim - 3)

    iy = lax.broadcasted_iota(jnp.int32, (rows_y, depth_z), 0)
    iz = lax.broadcasted_iota(jnp.int32, (rows_y, depth_z), 1)
    face_stack = jnp.stack(
        [
            perm_faces[0],
            perm_faces[1],
            jnp.where(iy < rows_y - 1, perm_faces[2], 0.0),
            jnp.where(iy > 0, perm_faces[3], 0.0),
            jnp.where(iz < depth_z - 1, perm_faces[4], 0.0),
            jnp.where(iz > 0, perm_faces[5], 0.0),
            storage + (
                perm_faces[0] + perm_faces[1] + perm_faces[2]
                + perm_faces[3] + perm_faces[4] + perm_faces[5]
            ),
        ]
    )
    mask_full = jnp.broadcast_to(mask_ext, (rows_ext, rows_y, depth_z))

    def solve(right_side, halo):
        lead = right_side.shape[:-3]
        flat_side = right_side.reshape((-1,) + right_side.shape[-3:])
        result = kernel_solve(
            flat_side, face_stack, mask_full, reach - halo, first, keeps, pushes
        )
        return result.reshape(lead + result.shape[-3:]), halo - CHEB

    def solve_xla(right_side, halo):
        solution = jnp.zeros_like(right_side)
        residual = right_side
        direction = right_side * first
        for turn in range(CHEB):
            face = tuple(part[reach - halo : reach + slab + halo - 2] for part in perm_faces)
            image = storage * inner(direction) + apply_faces(face, direction)
            solution = inner(solution) + inner(direction)
            residual = inner(residual) - image
            halo -= 1
            direction = (keeps[turn] * inner(direction) + pushes[turn] * residual) * rows_of(
                mask_ext, halo
            )
        return solution + direction, halo

    def begin(rech_ext, well_rows, rate_rows):
        hits = well_rows[:, :, None, None, None] == flat[None, None]
        points = jnp.sum(jnp.where(hits, rate_rows[:, :, None, None, None], 0.0), axis=1)
        own_hits = hits[:, :, reach : reach + slab]
        counts = jnp.sum(own_hits.astype(jnp.float32), axis=1)
        observe = gauge[None] + counts
        state, state_halo = solve(rech_ext + points, reach)
        forcing = -diffuse(rows_of(scaled_ext, state_halo)[None], state[:, None])
        forcing = forcing * rows_of(mask_ext, state_halo - 1)
        state = lax.slice_in_dim(state, CHEB, state.shape[1] - CHEB, axis=1)
        return state, forcing, observe

    parts_of = [begin(rech_own, wells, rates)]
    if tests > tests_here:
        parts_of.append(begin(rech_others, wells_others, rates_others))
    state, forcing, observe = (jnp.concatenate(group, axis=0) for group in zip(*parts_of))
    forcing = forcing.reshape(tests * cols, slab + 2 * CHEB, rows_y, depth_z)
    change, _ = solve(forcing, CHEB)
    weighted = (
        change.reshape(tests, cols, slab, rows_y, depth_z) * observe[:, None]
    ).reshape(tests * cols, slab, rows_y, depth_z)
    weighted_ext = with_halo(weighted, "cell", 1, CHEB + 1)
    adjoint, _ = solve(weighted_ext, CHEB + 1)
    adjoint = adjoint.reshape(tests, cols, slab + 2, rows_y, depth_z)
    contrib = jnp.sum(pairs(state[:, None], adjoint), axis=0)
    return -0.5 * perm[None] * contrib


def solution(mesh):
    return jax.shard_map(
        shards,
        mesh=mesh,
        in_specs=(
            P("cell", None, None),
            P("test", "cell", None, None),
            P("test", None),
            P("test", None),
            P("test", "cell", None, None),
            P("cell", None, None),
        ),
        out_specs=P("test", "cell", None, None),
        check_vma=False,
    )
```

```python
import functools
import math

import jax
import jax.numpy as jnp
from jax import lax
from jax.experimental import pallas as pl
from jax.experimental.pallas import tpu as pltpu
from jax.sharding import PartitionSpec as P


CHEB = 4


storage = 0.02


def with_halo(cells, axis, dim, width):
    count = lax.axis_size(axis)
    ends = count - 1
    head = lax.slice_in_dim(cells, 0, width, axis=dim)
    tail = lax.slice_in_dim(cells, cells.shape[dim] - width, cells.shape[dim], axis=dim)
    return jnp.concatenate(
        [
            lax.ppermute(tail, axis, [(i, i + 1) for i in range(ends)]),
            cells,
            lax.ppermute(head, axis, [(i + 1, i) for i in range(ends)]),
        ],
        axis=dim,
    )


INTERPRET = False


def solve_kernel(b_ref, k_ref, m_ref, o_ref, sol, res, da, db, *, offset, first, keeps, pushes):
    rows, rows_y, depth_z = sol.shape

    def init(r, c):
        da[r] = b_ref[0, r] * first
        return c

    lax.fori_loop(0, rows, init, 0, unroll=True)
    bufs = (da, db)
    for turn in range(CHEB):
        src = bufs[turn % 2]
        dst = bufs[(turn + 1) % 2]
        keep = keeps[turn]
        push = pushes[turn]

        def step(r, c, turn=turn, src=src, dst=dst, keep=keep, push=push):
            here = src[r]
            face = r - 1 + offset
            image = k_ref[6, face] * here - k_ref[0, face] * src[r + 1]
            image = image - k_ref[1, face] * src[r - 1]
            image = image - k_ref[2, face] * pltpu.roll(here, rows_y - 1, 0)
            image = image - k_ref[3, face] * pltpu.roll(here, 1, 0)
            image = image - k_ref[4, face] * pltpu.roll(here, depth_z - 1, 1)
            image = image - k_ref[5, face] * pltpu.roll(here, 1, 1)
            if turn == 0:
                summed = here
                fresh = b_ref[0, r] - image
            else:
                summed = sol[r] + here
                fresh = res[r] - image
            after = (keep * here + push * fresh) * m_ref[r + offset]
            if turn == CHEB - 1:
                o_ref[0, r - CHEB] = summed + after
            else:
                sol[r] = summed
                res[r] = fresh
                dst[r] = after
            return c

        lax.fori_loop(turn + 1, rows - 1 - turn, step, 0, unroll=True)


def kernel_solve(right_side, face_stack, mask_full, offset, first, keeps, pushes):
    fields, rows, rows_y, depth_z = right_side.shape
    body = functools.partial(
        solve_kernel,
        offset=offset,
        first=first,
        keeps=tuple(keeps),
        pushes=tuple(pushes),
    )
    return pl.pallas_call(
        body,
        grid=(fields,),
        in_specs=[
            pl.BlockSpec((1, rows, rows_y, depth_z), lambda f: (f, 0, 0, 0)),
            pl.BlockSpec(face_stack.shape, lambda f: (0, 0, 0, 0)),
            pl.BlockSpec(mask_full.shape, lambda f: (0, 0, 0)),
        ],
        out_specs=pl.BlockSpec((1, rows - 2 * CHEB, rows_y, depth_z), lambda f: (f, 0, 0, 0)),
        out_shape=jax.ShapeDtypeStruct((fields, rows - 2 * CHEB, rows_y, depth_z), jnp.float32),
        scratch_shapes=[pltpu.VMEM((rows, rows_y, depth_z), jnp.float32) for _ in range(4)],
        compiler_params=pltpu.CompilerParams(vmem_limit_bytes=48 * 1024 * 1024),
        interpret=INTERPRET,
    )(right_side, face_stack, mask_full)


def cheb_table(count):
    highest = storage + 12.0 * math.e
    theta = 0.5 * (highest + storage)
    spread = 0.5 * (highest - storage)
    sigma = theta / spread
    rho = 1.0 / sigma
    keeps = []
    pushes = []
    for _ in range(count):
        after = 1.0 / (2.0 * sigma - rho)
        keeps.append(after * rho)
        pushes.append(2.0 * after / spread)
        rho = after
    return (1.0 / theta, keeps, pushes)


def neighbours(field, back):
    axis = field.ndim - back
    widths = [(0, 0)] * field.ndim
    widths[axis] = (1, 1)
    padded = jnp.pad(field, widths)
    length = field.shape[axis]
    return (
        lax.slice_in_dim(padded, 2, length + 2, axis=axis),
        lax.slice_in_dim(padded, 0, length, axis=axis),
    )


def diffuse(weight_ext, field_ext):
    weight = weight_ext[..., 1:-1, :, :]
    field = field_ext[..., 1:-1, :, :]
    total = 0.5 * (weight + weight_ext[..., 2:, :, :]) * (field - field_ext[..., 2:, :, :])
    total = total + 0.5 * (weight + weight_ext[..., :-2, :, :]) * (
        field - field_ext[..., :-2, :, :]
    )
    for back in (2, 1):
        weight_up, weight_down = neighbours(weight, back)
        field_up, field_down = neighbours(field, back)
        total = (
            total
            + 0.5 * (weight + weight_up) * (field - field_up)
            + 0.5 * (weight + weight_down) * (field - field_down)
        )
    return total


def faces(weight_ext):
    weight = weight_ext[1:-1]
    weight_up_y, weight_down_y = neighbours(weight, 2)
    weight_up_z, weight_down_z = neighbours(weight, 1)
    return (
        0.5 * (weight + weight_ext[2:]),
        0.5 * (weight + weight_ext[:-2]),
        0.5 * (weight + weight_up_y),
        0.5 * (weight + weight_down_y),
        0.5 * (weight + weight_up_z),
        0.5 * (weight + weight_down_z),
    )


def pairs(left_ext, right_ext):
    left = left_ext[..., 1:-1, :, :]
    right = right_ext[..., 1:-1, :, :]
    total = (left - left_ext[..., 2:, :, :]) * (right - right_ext[..., 2:, :, :])
    total = total + (left - left_ext[..., :-2, :, :]) * (right - right_ext[..., :-2, :, :])
    for back in (2, 1):
        left_up, left_down = neighbours(left, back)
        right_up, right_down = neighbours(right, back)
        total = (
            total
            + (left - left_up) * (right - right_up)
            + (left - left_down) * (right - right_down)
        )
    return total


def shards(log_perm, panel, wells, rates, recharge, gauge):
    place = lax.axis_index("cell")
    parts = lax.axis_size("cell")
    slab, rows_y, depth_z = log_perm.shape
    cols = panel.shape[0]
    tests_here, well_count = wells.shape
    first, keeps, pushes = cheb_table(CHEB)
    reach = 2 * CHEB + 1
    rows_ext = slab + 2 * reach
    perm = jnp.exp(log_perm)
    scaled = perm[None] * panel
    stacked = jnp.concatenate([perm[None], scaled, recharge], axis=0)
    ext = with_halo(stacked, "cell", 1, reach)
    perm_ext = ext[0]
    scaled_ext = ext[1 : 1 + cols]
    rech_own = ext[1 + cols :]
    cells = slab * rows_y * depth_z
    packed = jnp.concatenate(
        [recharge.reshape(tests_here, cells), wells.astype(jnp.float32), rates], axis=1
    )
    groups = lax.axis_size("test")
    tests = groups * tests_here
    others = jnp.concatenate(
        [
            lax.ppermute(packed, "test", [(i, (i + shift) % groups) for i in range(groups)])
            for shift in range(1, groups)
        ]
        or [packed[:0]],
        axis=0,
    )
    rech_others = with_halo(
        others[:, :cells].reshape(tests - tests_here, slab, rows_y, depth_z), "cell", 1, reach
    )
    wells_others = others[:, cells : cells + well_count].astype(jnp.int32)
    rates_others = others[:, cells + well_count :]

    gx = place * slab - reach + jnp.arange(rows_ext, dtype=jnp.int32)
    mask_ext = ((gx >= 0) & (gx < parts * slab)).astype(jnp.float32)[:, None, None]
    flat = (
        gx[:, None, None] * (rows_y * depth_z)
        + jnp.arange(rows_y, dtype=jnp.int32)[None, :, None] * depth_z
        + jnp.arange(depth_z, dtype=jnp.int32)[None, None, :]
    )

    perm_faces = faces(perm_ext)

    def rows_of(field, halo):
        return lax.slice_in_dim(field, reach - halo, reach + slab + halo, axis=field.ndim - 3)

    iy = lax.broadcasted_iota(jnp.int32, (rows_y, depth_z), 0)
    iz = lax.broadcasted_iota(jnp.int32, (rows_y, depth_z), 1)
    face_stack = jnp.stack(
        [
            perm_faces[0],
            perm_faces[1],
            jnp.where(iy < rows_y - 1, perm_faces[2], 0.0),
            jnp.where(iy > 0, perm_faces[3], 0.0),
            jnp.where(iz < depth_z - 1, perm_faces[4], 0.0),
            jnp.where(iz > 0, perm_faces[5], 0.0),
            storage + (
                perm_faces[0] + perm_faces[1] + perm_faces[2]
                + perm_faces[3] + perm_faces[4] + perm_faces[5]
            ),
        ]
    )
    mask_full = jnp.broadcast_to(mask_ext, (rows_ext, rows_y, depth_z))

    def solve(right_side, halo):
        lead = right_side.shape[:-3]
        flat_side = right_side.reshape((-1,) + right_side.shape[-3:])
        result = kernel_solve(
            flat_side, face_stack, mask_full, reach - halo, first, keeps, pushes
        )
        return result.reshape(lead + result.shape[-3:]), halo - CHEB

    def begin(rech_ext, well_rows, rate_rows):
        hits = well_rows[:, :, None, None, None] == flat[None, None]
        points = jnp.sum(jnp.where(hits, rate_rows[:, :, None, None, None], 0.0), axis=1)
        own_hits = hits[:, :, reach : reach + slab]
        counts = jnp.sum(own_hits.astype(jnp.float32), axis=1)
        observe = gauge[None] + counts
        state, state_halo = solve(rech_ext + points, reach)
        forcing = -diffuse(rows_of(scaled_ext, state_halo)[None], state[:, None])
        forcing = forcing * rows_of(mask_ext, state_halo - 1)
        state = lax.slice_in_dim(state, CHEB, state.shape[1] - CHEB, axis=1)
        return state, forcing, observe

    parts_of = [begin(rech_own, wells, rates)]
    if tests > tests_here:
        parts_of.append(begin(rech_others, wells_others, rates_others))
    state, forcing, observe = (jnp.concatenate(group, axis=0) for group in zip(*parts_of))
    forcing = forcing.reshape(tests * cols, slab + 2 * CHEB, rows_y, depth_z)
    fields = tests * cols
    observe_fields = jnp.broadcast_to(
        observe[:, None], (tests, cols, slab, rows_y, depth_z)
    ).reshape(fields, slab, rows_y, depth_z)
    half = fields // 2
    spans = [(0, half), (half, fields)] if half else [(0, fields)]
    halos = []
    ahead = forcing[spans[0][0] : spans[0][1]]
    for index, (lo, hi) in enumerate(spans):
        change, _ = solve(ahead, CHEB)
        weighted = change * observe_fields[lo:hi]
        if index + 1 < len(spans):
            nxt = spans[index + 1]
            weighted, ahead = lax.optimization_barrier((weighted, forcing[nxt[0] : nxt[1]]))
        halos.append(with_halo(weighted, "cell", 1, CHEB + 1))
    adjoints = []
    for part in halos:
        adjoints.append(solve(part, CHEB + 1)[0])
    adjoint = jnp.concatenate(adjoints, axis=0)
    adjoint = adjoint.reshape(tests, cols, slab + 2, rows_y, depth_z)
    contrib = jnp.sum(pairs(state[:, None], adjoint), axis=0)
    return -0.5 * perm[None] * contrib


def solution(mesh):
    return jax.shard_map(
        shards,
        mesh=mesh,
        in_specs=(
            P("cell", None, None),
            P("test", "cell", None, None),
            P("test", None),
            P("test", None),
            P("test", "cell", None, None),
            P("cell", None, None),
        ),
        out_specs=P("test", "cell", None, None),
        check_vma=False,
    )
```

```python
import functools
import math

import jax
import jax.numpy as jnp
from jax import lax
from jax.experimental import pallas as pl
from jax.experimental.pallas import tpu as pltpu
from jax.sharding import PartitionSpec as P


CHEB = 4


storage = 0.02


def with_halo(cells, axis, dim, width):
    count = lax.axis_size(axis)
    ends = count - 1
    head = lax.slice_in_dim(cells, 0, width, axis=dim)
    tail = lax.slice_in_dim(cells, cells.shape[dim] - width, cells.shape[dim], axis=dim)
    return jnp.concatenate(
        [
            lax.ppermute(tail, axis, [(i, i + 1) for i in range(ends)]),
            cells,
            lax.ppermute(head, axis, [(i + 1, i) for i in range(ends)]),
        ],
        axis=dim,
    )


INTERPRET = False


def solve_kernel(b_ref, k_ref, m_ref, o_ref, sol, res, da, db, *, offset, first, keeps, pushes):
    block, rows, rows_y, depth_z = sol.shape

    def init(r, c):
        da[:, r] = b_ref[:, r] * first
        return c

    lax.fori_loop(0, rows, init, 0, unroll=True)
    bufs = (da, db)
    for turn in range(CHEB):
        src = bufs[turn % 2]
        dst = bufs[(turn + 1) % 2]
        keep = keeps[turn]
        push = pushes[turn]

        def step(r, c, turn=turn, src=src, dst=dst, keep=keep, push=push):
            face = r - 1 + offset
            coeff = [k_ref[j, face] for j in range(7)]
            gate = m_ref[r + offset]
            for f in range(block):
                here = src[f, r]
                image = coeff[6] * here - coeff[0] * src[f, r + 1]
                image = image - coeff[1] * src[f, r - 1]
                image = image - coeff[2] * pltpu.roll(here, rows_y - 1, 0)
                image = image - coeff[3] * pltpu.roll(here, 1, 0)
                image = image - coeff[4] * pltpu.roll(here, depth_z - 1, 1)
                image = image - coeff[5] * pltpu.roll(here, 1, 1)
                if turn == 0:
                    summed = here
                    fresh = b_ref[f, r] - image
                else:
                    summed = sol[f, r] + here
                    fresh = res[f, r] - image
                after = (keep * here + push * fresh) * gate
                if turn == CHEB - 1:
                    o_ref[f, r - CHEB] = summed + after
                else:
                    sol[f, r] = summed
                    res[f, r] = fresh
                    dst[f, r] = after
            return c

        lax.fori_loop(turn + 1, rows - 1 - turn, step, 0, unroll=True)


def kernel_solve(right_side, face_stack, mask_full, offset, first, keeps, pushes):
    fields, rows, rows_y, depth_z = right_side.shape
    block = 2 if fields % 2 == 0 else 1
    body = functools.partial(
        solve_kernel,
        offset=offset,
        first=first,
        keeps=tuple(keeps),
        pushes=tuple(pushes),
    )
    return pl.pallas_call(
        body,
        grid=(fields // block,),
        in_specs=[
            pl.BlockSpec((block, rows, rows_y, depth_z), lambda f: (f, 0, 0, 0)),
            pl.BlockSpec(face_stack.shape, lambda f: (0, 0, 0, 0)),
            pl.BlockSpec(mask_full.shape, lambda f: (0, 0, 0)),
        ],
        out_specs=pl.BlockSpec((block, rows - 2 * CHEB, rows_y, depth_z), lambda f: (f, 0, 0, 0)),
        out_shape=jax.ShapeDtypeStruct((fields, rows - 2 * CHEB, rows_y, depth_z), jnp.float32),
        scratch_shapes=[
            pltpu.VMEM((block, rows, rows_y, depth_z), jnp.float32) for _ in range(4)
        ],
        compiler_params=pltpu.CompilerParams(vmem_limit_bytes=48 * 1024 * 1024),
        interpret=INTERPRET,
    )(right_side, face_stack, mask_full)


def cheb_table(count):
    highest = storage + 12.0 * math.e
    theta = 0.5 * (highest + storage)
    spread = 0.5 * (highest - storage)
    sigma = theta / spread
    rho = 1.0 / sigma
    keeps = []
    pushes = []
    for _ in range(count):
        after = 1.0 / (2.0 * sigma - rho)
        keeps.append(after * rho)
        pushes.append(2.0 * after / spread)
        rho = after
    return (1.0 / theta, keeps, pushes)


def neighbours(field, back):
    axis = field.ndim - back
    widths = [(0, 0)] * field.ndim
    widths[axis] = (1, 1)
    padded = jnp.pad(field, widths)
    length = field.shape[axis]
    return (
        lax.slice_in_dim(padded, 2, length + 2, axis=axis),
        lax.slice_in_dim(padded, 0, length, axis=axis),
    )


def diffuse(weight_ext, field_ext):
    weight = weight_ext[..., 1:-1, :, :]
    field = field_ext[..., 1:-1, :, :]
    total = 0.5 * (weight + weight_ext[..., 2:, :, :]) * (field - field_ext[..., 2:, :, :])
    total = total + 0.5 * (weight + weight_ext[..., :-2, :, :]) * (
        field - field_ext[..., :-2, :, :]
    )
    for back in (2, 1):
        weight_up, weight_down = neighbours(weight, back)
        field_up, field_down = neighbours(field, back)
        total = (
            total
            + 0.5 * (weight + weight_up) * (field - field_up)
            + 0.5 * (weight + weight_down) * (field - field_down)
        )
    return total


def faces(weight_ext):
    weight = weight_ext[1:-1]
    weight_up_y, weight_down_y = neighbours(weight, 2)
    weight_up_z, weight_down_z = neighbours(weight, 1)
    return (
        0.5 * (weight + weight_ext[2:]),
        0.5 * (weight + weight_ext[:-2]),
        0.5 * (weight + weight_up_y),
        0.5 * (weight + weight_down_y),
        0.5 * (weight + weight_up_z),
        0.5 * (weight + weight_down_z),
    )


def pairs(left_ext, right_ext):
    left = left_ext[..., 1:-1, :, :]
    right = right_ext[..., 1:-1, :, :]
    total = (left - left_ext[..., 2:, :, :]) * (right - right_ext[..., 2:, :, :])
    total = total + (left - left_ext[..., :-2, :, :]) * (right - right_ext[..., :-2, :, :])
    for back in (2, 1):
        left_up, left_down = neighbours(left, back)
        right_up, right_down = neighbours(right, back)
        total = (
            total
            + (left - left_up) * (right - right_up)
            + (left - left_down) * (right - right_down)
        )
    return total


def shards(log_perm, panel, wells, rates, recharge, gauge):
    place = lax.axis_index("cell")
    parts = lax.axis_size("cell")
    slab, rows_y, depth_z = log_perm.shape
    cols = panel.shape[0]
    tests_here, well_count = wells.shape
    first, keeps, pushes = cheb_table(CHEB)
    reach = 2 * CHEB + 1
    rows_ext = slab + 2 * reach
    perm = jnp.exp(log_perm)
    scaled = perm[None] * panel
    stacked = jnp.concatenate([perm[None], scaled, recharge], axis=0)
    ext = with_halo(stacked, "cell", 1, reach)
    perm_ext = ext[0]
    scaled_ext = ext[1 : 1 + cols]
    rech_own = ext[1 + cols :]
    cells = slab * rows_y * depth_z
    packed = jnp.concatenate(
        [recharge.reshape(tests_here, cells), wells.astype(jnp.float32), rates], axis=1
    )
    groups = lax.axis_size("test")
    tests = groups * tests_here
    others = jnp.concatenate(
        [
            lax.ppermute(packed, "test", [(i, (i + shift) % groups) for i in range(groups)])
            for shift in range(1, groups)
        ]
        or [packed[:0]],
        axis=0,
    )
    rech_others = with_halo(
        others[:, :cells].reshape(tests - tests_here, slab, rows_y, depth_z), "cell", 1, reach
    )
    wells_others = others[:, cells : cells + well_count].astype(jnp.int32)
    rates_others = others[:, cells + well_count :]

    gx = place * slab - reach + jnp.arange(rows_ext, dtype=jnp.int32)
    mask_ext = ((gx >= 0) & (gx < parts * slab)).astype(jnp.float32)[:, None, None]
    flat = (
        gx[:, None, None] * (rows_y * depth_z)
        + jnp.arange(rows_y, dtype=jnp.int32)[None, :, None] * depth_z
        + jnp.arange(depth_z, dtype=jnp.int32)[None, None, :]
    )

    perm_faces = faces(perm_ext)

    def rows_of(field, halo):
        return lax.slice_in_dim(field, reach - halo, reach + slab + halo, axis=field.ndim - 3)

    iy = lax.broadcasted_iota(jnp.int32, (rows_y, depth_z), 0)
    iz = lax.broadcasted_iota(jnp.int32, (rows_y, depth_z), 1)
    face_stack = jnp.stack(
        [
            perm_faces[0],
            perm_faces[1],
            jnp.where(iy < rows_y - 1, perm_faces[2], 0.0),
            jnp.where(iy > 0, perm_faces[3], 0.0),
            jnp.where(iz < depth_z - 1, perm_faces[4], 0.0),
            jnp.where(iz > 0, perm_faces[5], 0.0),
            storage + (
                perm_faces[0] + perm_faces[1] + perm_faces[2]
                + perm_faces[3] + perm_faces[4] + perm_faces[5]
            ),
        ]
    )
    mask_full = jnp.broadcast_to(mask_ext, (rows_ext, rows_y, depth_z))

    def solve(right_side, halo):
        lead = right_side.shape[:-3]
        flat_side = right_side.reshape((-1,) + right_side.shape[-3:])
        result = kernel_solve(
            flat_side, face_stack, mask_full, reach - halo, first, keeps, pushes
        )
        return result.reshape(lead + result.shape[-3:]), halo - CHEB

    def begin(rech_ext, well_rows, rate_rows):
        hits = well_rows[:, :, None, None, None] == flat[None, None]
        points = jnp.sum(jnp.where(hits, rate_rows[:, :, None, None, None], 0.0), axis=1)
        own_hits = hits[:, :, reach : reach + slab]
        counts = jnp.sum(own_hits.astype(jnp.float32), axis=1)
        observe = gauge[None] + counts
        state, state_halo = solve(rech_ext + points, reach)
        forcing = -diffuse(rows_of(scaled_ext, state_halo)[None], state[:, None])
        forcing = forcing * rows_of(mask_ext, state_halo - 1)
        state = lax.slice_in_dim(state, CHEB, state.shape[1] - CHEB, axis=1)
        return state, forcing, observe

    parts_of = [begin(rech_own, wells, rates)]
    if tests > tests_here:
        parts_of.append(begin(rech_others, wells_others, rates_others))
    state, forcing, observe = (jnp.concatenate(group, axis=0) for group in zip(*parts_of))
    forcing = forcing.reshape(tests * cols, slab + 2 * CHEB, rows_y, depth_z)
    fields = tests * cols
    observe_fields = jnp.broadcast_to(
        observe[:, None], (tests, cols, slab, rows_y, depth_z)
    ).reshape(fields, slab, rows_y, depth_z)
    half = fields // 2
    spans = [(0, half), (half, fields)] if half else [(0, fields)]
    halos = []
    ahead = forcing[spans[0][0] : spans[0][1]]
    for index, (lo, hi) in enumerate(spans):
        change, _ = solve(ahead, CHEB)
        weighted = change * observe_fields[lo:hi]
        if index + 1 < len(spans):
            nxt = spans[index + 1]
            weighted, ahead = lax.optimization_barrier((weighted, forcing[nxt[0] : nxt[1]]))
        halos.append(with_halo(weighted, "cell", 1, CHEB + 1))
    adjoints = []
    for part in halos:
        adjoints.append(solve(part, CHEB + 1)[0])
    adjoint = jnp.concatenate(adjoints, axis=0)
    adjoint = adjoint.reshape(tests, cols, slab + 2, rows_y, depth_z)
    contrib = jnp.sum(pairs(state[:, None], adjoint), axis=0)
    return -0.5 * perm[None] * contrib


def solution(mesh):
    return jax.shard_map(
        shards,
        mesh=mesh,
        in_specs=(
            P("cell", None, None),
            P("test", "cell", None, None),
            P("test", None),
            P("test", None),
            P("test", "cell", None, None),
            P("cell", None, None),
        ),
        out_specs=P("test", "cell", None, None),
        check_vma=False,
    )
```

```python
import functools
import math

import jax
import jax.numpy as jnp
from jax import lax
from jax.experimental import pallas as pl
from jax.experimental.pallas import tpu as pltpu
from jax.sharding import PartitionSpec as P


CHEB = 4


storage = 0.02


def with_halo(cells, axis, dim, width):
    count = lax.axis_size(axis)
    ends = count - 1
    head = lax.slice_in_dim(cells, 0, width, axis=dim)
    tail = lax.slice_in_dim(cells, cells.shape[dim] - width, cells.shape[dim], axis=dim)
    return jnp.concatenate(
        [
            lax.ppermute(tail, axis, [(i, i + 1) for i in range(ends)]),
            cells,
            lax.ppermute(head, axis, [(i + 1, i) for i in range(ends)]),
        ],
        axis=dim,
    )


INTERPRET = False


def solve_kernel(b_ref, k_ref, m_ref, o_ref, sol, res, da, db, *, offset, first, keeps, pushes):
    block, rows, rows_y, depth_z = sol.shape

    def init(r, c):
        da[:, r] = b_ref[:, r] * first
        return c

    lax.fori_loop(0, rows, init, 0, unroll=True)
    bufs = (da, db)
    for turn in range(CHEB):
        src = bufs[turn % 2]
        dst = bufs[(turn + 1) % 2]
        keep = keeps[turn]
        push = pushes[turn]

        def step(r, c, turn=turn, src=src, dst=dst, keep=keep, push=push):
            face = r - 1 + offset
            coeff = [k_ref[j, face] for j in range(7)]
            for f in range(block):
                here = src[f, r]
                image = coeff[6] * here - coeff[0] * src[f, r + 1]
                image = image - coeff[1] * src[f, r - 1]
                image = image - coeff[2] * pltpu.roll(here, rows_y - 1, 0)
                image = image - coeff[3] * pltpu.roll(here, 1, 0)
                image = image - coeff[4] * pltpu.roll(here, depth_z - 1, 1)
                image = image - coeff[5] * pltpu.roll(here, 1, 1)
                if turn == 0:
                    summed = here
                    fresh = b_ref[f, r] - image
                else:
                    summed = sol[f, r] + here
                    fresh = res[f, r] - image
                after = keep * here + push * fresh
                if turn == CHEB - 1:
                    o_ref[f, r - CHEB] = summed + after
                else:
                    sol[f, r] = summed
                    res[f, r] = fresh
                    dst[f, r] = after
            return c

        lax.fori_loop(turn + 1, rows - 1 - turn, step, 0, unroll=True)


def kernel_solve(right_side, face_stack, mask_full, offset, first, keeps, pushes):
    fields, rows, rows_y, depth_z = right_side.shape
    block = 2 if fields % 2 == 0 else 1
    body = functools.partial(
        solve_kernel,
        offset=offset,
        first=first,
        keeps=tuple(keeps),
        pushes=tuple(pushes),
    )
    return pl.pallas_call(
        body,
        grid=(fields // block,),
        in_specs=[
            pl.BlockSpec((block, rows, rows_y, depth_z), lambda f: (f, 0, 0, 0)),
            pl.BlockSpec(face_stack.shape, lambda f: (0, 0, 0, 0)),
            pl.BlockSpec(mask_full.shape, lambda f: (0, 0, 0)),
        ],
        out_specs=pl.BlockSpec((block, rows - 2 * CHEB, rows_y, depth_z), lambda f: (f, 0, 0, 0)),
        out_shape=jax.ShapeDtypeStruct((fields, rows - 2 * CHEB, rows_y, depth_z), jnp.float32),
        scratch_shapes=[
            pltpu.VMEM((block, rows, rows_y, depth_z), jnp.float32) for _ in range(4)
        ],
        compiler_params=pltpu.CompilerParams(vmem_limit_bytes=48 * 1024 * 1024),
        interpret=INTERPRET,
    )(right_side, face_stack, mask_full)


def cheb_table(count):
    highest = storage + 12.0 * math.e
    theta = 0.5 * (highest + storage)
    spread = 0.5 * (highest - storage)
    sigma = theta / spread
    rho = 1.0 / sigma
    keeps = []
    pushes = []
    for _ in range(count):
        after = 1.0 / (2.0 * sigma - rho)
        keeps.append(after * rho)
        pushes.append(2.0 * after / spread)
        rho = after
    return (1.0 / theta, keeps, pushes)


def neighbours(field, back):
    axis = field.ndim - back
    widths = [(0, 0)] * field.ndim
    widths[axis] = (1, 1)
    padded = jnp.pad(field, widths)
    length = field.shape[axis]
    return (
        lax.slice_in_dim(padded, 2, length + 2, axis=axis),
        lax.slice_in_dim(padded, 0, length, axis=axis),
    )


def diffuse(weight_ext, field_ext):
    weight = weight_ext[..., 1:-1, :, :]
    field = field_ext[..., 1:-1, :, :]
    total = 0.5 * (weight + weight_ext[..., 2:, :, :]) * (field - field_ext[..., 2:, :, :])
    total = total + 0.5 * (weight + weight_ext[..., :-2, :, :]) * (
        field - field_ext[..., :-2, :, :]
    )
    for back in (2, 1):
        weight_up, weight_down = neighbours(weight, back)
        field_up, field_down = neighbours(field, back)
        total = (
            total
            + 0.5 * (weight + weight_up) * (field - field_up)
            + 0.5 * (weight + weight_down) * (field - field_down)
        )
    return total


def faces(weight_ext):
    weight = weight_ext[1:-1]
    weight_up_y, weight_down_y = neighbours(weight, 2)
    weight_up_z, weight_down_z = neighbours(weight, 1)
    return (
        0.5 * (weight + weight_ext[2:]),
        0.5 * (weight + weight_ext[:-2]),
        0.5 * (weight + weight_up_y),
        0.5 * (weight + weight_down_y),
        0.5 * (weight + weight_up_z),
        0.5 * (weight + weight_down_z),
    )


def pairs(left_ext, right_ext):
    left = left_ext[..., 1:-1, :, :]
    right = right_ext[..., 1:-1, :, :]
    total = (left - left_ext[..., 2:, :, :]) * (right - right_ext[..., 2:, :, :])
    total = total + (left - left_ext[..., :-2, :, :]) * (right - right_ext[..., :-2, :, :])
    for back in (2, 1):
        left_up, left_down = neighbours(left, back)
        right_up, right_down = neighbours(right, back)
        total = (
            total
            + (left - left_up) * (right - right_up)
            + (left - left_down) * (right - right_down)
        )
    return total


def shards(log_perm, panel, wells, rates, recharge, gauge):
    place = lax.axis_index("cell")
    parts = lax.axis_size("cell")
    slab, rows_y, depth_z = log_perm.shape
    cols = panel.shape[0]
    tests_here, well_count = wells.shape
    first, keeps, pushes = cheb_table(CHEB)
    reach = 2 * CHEB + 1
    rows_ext = slab + 2 * reach
    perm = jnp.exp(log_perm)
    scaled = perm[None] * panel
    stacked = jnp.concatenate([perm[None], scaled, recharge], axis=0)
    ext = with_halo(stacked, "cell", 1, reach)
    perm_ext = ext[0]
    scaled_ext = ext[1 : 1 + cols]
    rech_own = ext[1 + cols :]
    cells = slab * rows_y * depth_z
    packed = jnp.concatenate(
        [recharge.reshape(tests_here, cells), wells.astype(jnp.float32), rates], axis=1
    )
    groups = lax.axis_size("test")
    tests = groups * tests_here
    others = jnp.concatenate(
        [
            lax.ppermute(packed, "test", [(i, (i + shift) % groups) for i in range(groups)])
            for shift in range(1, groups)
        ]
        or [packed[:0]],
        axis=0,
    )
    rech_others = with_halo(
        others[:, :cells].reshape(tests - tests_here, slab, rows_y, depth_z), "cell", 1, reach
    )
    wells_others = others[:, cells : cells + well_count].astype(jnp.int32)
    rates_others = others[:, cells + well_count :]

    gx = place * slab - reach + jnp.arange(rows_ext, dtype=jnp.int32)
    mask_ext = ((gx >= 0) & (gx < parts * slab)).astype(jnp.float32)[:, None, None]
    flat = (
        gx[:, None, None] * (rows_y * depth_z)
        + jnp.arange(rows_y, dtype=jnp.int32)[None, :, None] * depth_z
        + jnp.arange(depth_z, dtype=jnp.int32)[None, None, :]
    )

    perm_faces = faces(perm_ext)

    def rows_of(field, halo):
        return lax.slice_in_dim(field, reach - halo, reach + slab + halo, axis=field.ndim - 3)

    iy = lax.broadcasted_iota(jnp.int32, (rows_y, depth_z), 0)
    iz = lax.broadcasted_iota(jnp.int32, (rows_y, depth_z), 1)
    face_stack = jnp.stack(
        [
            perm_faces[0],
            perm_faces[1],
            jnp.where(iy < rows_y - 1, perm_faces[2], 0.0),
            jnp.where(iy > 0, perm_faces[3], 0.0),
            jnp.where(iz < depth_z - 1, perm_faces[4], 0.0),
            jnp.where(iz > 0, perm_faces[5], 0.0),
            storage + (
                perm_faces[0] + perm_faces[1] + perm_faces[2]
                + perm_faces[3] + perm_faces[4] + perm_faces[5]
            ),
        ]
    ) * mask_ext[None, 1:-1]
    mask_full = jnp.broadcast_to(mask_ext, (rows_ext, rows_y, depth_z))

    def solve(right_side, halo):
        lead = right_side.shape[:-3]
        flat_side = right_side.reshape((-1,) + right_side.shape[-3:])
        result = kernel_solve(
            flat_side, face_stack, mask_full, reach - halo, first, keeps, pushes
        )
        return result.reshape(lead + result.shape[-3:]), halo - CHEB

    def begin(rech_ext, well_rows, rate_rows):
        hits = well_rows[:, :, None, None, None] == flat[None, None]
        points = jnp.sum(jnp.where(hits, rate_rows[:, :, None, None, None], 0.0), axis=1)
        own_hits = hits[:, :, reach : reach + slab]
        counts = jnp.sum(own_hits.astype(jnp.float32), axis=1)
        observe = gauge[None] + counts
        state, state_halo = solve(rech_ext + points, reach)
        forcing = -diffuse(rows_of(scaled_ext, state_halo)[None], state[:, None])
        forcing = forcing * rows_of(mask_ext, state_halo - 1)
        state = lax.slice_in_dim(state, CHEB, state.shape[1] - CHEB, axis=1)
        return state, forcing, observe

    parts_of = [begin(rech_own, wells, rates)]
    if tests > tests_here:
        parts_of.append(begin(rech_others, wells_others, rates_others))
    state, forcing, observe = (jnp.concatenate(group, axis=0) for group in zip(*parts_of))
    forcing = forcing.reshape(tests * cols, slab + 2 * CHEB, rows_y, depth_z)
    fields = tests * cols
    observe_fields = jnp.broadcast_to(
        observe[:, None], (tests, cols, slab, rows_y, depth_z)
    ).reshape(fields, slab, rows_y, depth_z)
    half = fields // 2
    spans = [(0, half), (half, fields)] if half else [(0, fields)]
    halos = []
    ahead = forcing[spans[0][0] : spans[0][1]]
    for index, (lo, hi) in enumerate(spans):
        change, _ = solve(ahead, CHEB)
        weighted = change * observe_fields[lo:hi]
        if index + 1 < len(spans):
            nxt = spans[index + 1]
            weighted, ahead = lax.optimization_barrier((weighted, forcing[nxt[0] : nxt[1]]))
        halos.append(with_halo(weighted, "cell", 1, CHEB + 1))
    adjoints = []
    for part in halos:
        adjoints.append(solve(part, CHEB + 1)[0])
    adjoint = jnp.concatenate(adjoints, axis=0)
    adjoint = adjoint.reshape(tests, cols, slab + 2, rows_y, depth_z)
    contrib = jnp.sum(pairs(state[:, None], adjoint), axis=0)
    return -0.5 * perm[None] * contrib


def solution(mesh):
    return jax.shard_map(
        shards,
        mesh=mesh,
        in_specs=(
            P("cell", None, None),
            P("test", "cell", None, None),
            P("test", None),
            P("test", None),
            P("test", "cell", None, None),
            P("cell", None, None),
        ),
        out_specs=P("test", "cell", None, None),
        check_vma=False,
    )
```

```python
import functools
import math

import jax
import jax.numpy as jnp
from jax import lax
from jax.experimental import pallas as pl
from jax.experimental.pallas import tpu as pltpu
from jax.sharding import PartitionSpec as P


CHEB = 4


storage = 0.02


def with_halo(cells, axis, dim, width):
    count = lax.axis_size(axis)
    ends = count - 1
    head = lax.slice_in_dim(cells, 0, width, axis=dim)
    tail = lax.slice_in_dim(cells, cells.shape[dim] - width, cells.shape[dim], axis=dim)
    return jnp.concatenate(
        [
            lax.ppermute(tail, axis, [(i, i + 1) for i in range(ends)]),
            cells,
            lax.ppermute(head, axis, [(i + 1, i) for i in range(ends)]),
        ],
        axis=dim,
    )


INTERPRET = False


def solve_kernel(b_ref, k_ref, o_ref, sol, res, da, db, *, offset, first, keeps, pushes):
    block, rows, rows_y, depth_z = sol.shape

    def init(r, c):
        da[:, r] = b_ref[:, r] * first
        return c

    lax.fori_loop(0, rows, init, 0, unroll=True)
    bufs = (da, db)
    for turn in range(CHEB):
        src = bufs[turn % 2]
        dst = bufs[(turn + 1) % 2]
        keep = keeps[turn]
        push = pushes[turn]

        def step(r, c, turn=turn, src=src, dst=dst, keep=keep, push=push):
            face = r - 1 + offset
            coeff = [k_ref[j, face] for j in range(7)]
            for f in range(block):
                here = src[f, r]
                image = coeff[6] * here - coeff[0] * src[f, r + 1]
                image = image - coeff[1] * src[f, r - 1]
                image = image - coeff[2] * pltpu.roll(here, rows_y - 1, 0)
                image = image - coeff[3] * pltpu.roll(here, 1, 0)
                image = image - coeff[4] * pltpu.roll(here, depth_z - 1, 1)
                image = image - coeff[5] * pltpu.roll(here, 1, 1)
                if turn == 0:
                    summed = here
                    fresh = b_ref[f, r] - image
                else:
                    summed = sol[f, r] + here
                    fresh = res[f, r] - image
                after = keep * here + push * fresh
                if turn == CHEB - 1:
                    o_ref[f, r - CHEB] = summed + after
                else:
                    sol[f, r] = summed
                    res[f, r] = fresh
                    dst[f, r] = after
            return c

        lax.fori_loop(turn + 1, rows - 1 - turn, step, 0, unroll=True)


def kernel_solve(right_side, face_stack, offset, first, keeps, pushes):
    fields, rows, rows_y, depth_z = right_side.shape
    block = 2 if fields % 2 == 0 else 1
    body = functools.partial(
        solve_kernel,
        offset=offset,
        first=first,
        keeps=tuple(keeps),
        pushes=tuple(pushes),
    )
    return pl.pallas_call(
        body,
        grid=(fields // block,),
        in_specs=[
            pl.BlockSpec((block, rows, rows_y, depth_z), lambda f: (f, 0, 0, 0)),
            pl.BlockSpec(face_stack.shape, lambda f: (0, 0, 0, 0)),
        ],
        out_specs=pl.BlockSpec((block, rows - 2 * CHEB, rows_y, depth_z), lambda f: (f, 0, 0, 0)),
        out_shape=jax.ShapeDtypeStruct((fields, rows - 2 * CHEB, rows_y, depth_z), jnp.float32),
        scratch_shapes=[
            pltpu.VMEM((block, rows, rows_y, depth_z), jnp.float32) for _ in range(4)
        ],
        compiler_params=pltpu.CompilerParams(vmem_limit_bytes=48 * 1024 * 1024),
        interpret=INTERPRET,
    )(right_side, face_stack)


def cheb_table(count):
    highest = storage + 12.0 * math.e
    theta = 0.5 * (highest + storage)
    spread = 0.5 * (highest - storage)
    sigma = theta / spread
    rho = 1.0 / sigma
    keeps = []
    pushes = []
    for _ in range(count):
        after = 1.0 / (2.0 * sigma - rho)
        keeps.append(after * rho)
        pushes.append(2.0 * after / spread)
        rho = after
    return (1.0 / theta, keeps, pushes)


def neighbours(field, back):
    axis = field.ndim - back
    widths = [(0, 0)] * field.ndim
    widths[axis] = (1, 1)
    padded = jnp.pad(field, widths)
    length = field.shape[axis]
    return (
        lax.slice_in_dim(padded, 2, length + 2, axis=axis),
        lax.slice_in_dim(padded, 0, length, axis=axis),
    )


def diffuse(weight_ext, field_ext):
    weight = weight_ext[..., 1:-1, :, :]
    field = field_ext[..., 1:-1, :, :]
    total = 0.5 * (weight + weight_ext[..., 2:, :, :]) * (field - field_ext[..., 2:, :, :])
    total = total + 0.5 * (weight + weight_ext[..., :-2, :, :]) * (
        field - field_ext[..., :-2, :, :]
    )
    for back in (2, 1):
        weight_up, weight_down = neighbours(weight, back)
        field_up, field_down = neighbours(field, back)
        total = (
            total
            + 0.5 * (weight + weight_up) * (field - field_up)
            + 0.5 * (weight + weight_down) * (field - field_down)
        )
    return total


def faces(weight_ext):
    weight = weight_ext[1:-1]
    weight_up_y, weight_down_y = neighbours(weight, 2)
    weight_up_z, weight_down_z = neighbours(weight, 1)
    return (
        0.5 * (weight + weight_ext[2:]),
        0.5 * (weight + weight_ext[:-2]),
        0.5 * (weight + weight_up_y),
        0.5 * (weight + weight_down_y),
        0.5 * (weight + weight_up_z),
        0.5 * (weight + weight_down_z),
    )


def pairs(left_ext, right_ext):
    left = left_ext[..., 1:-1, :, :]
    right = right_ext[..., 1:-1, :, :]
    total = (left - left_ext[..., 2:, :, :]) * (right - right_ext[..., 2:, :, :])
    total = total + (left - left_ext[..., :-2, :, :]) * (right - right_ext[..., :-2, :, :])
    for back in (2, 1):
        left_up, left_down = neighbours(left, back)
        right_up, right_down = neighbours(right, back)
        total = (
            total
            + (left - left_up) * (right - right_up)
            + (left - left_down) * (right - right_down)
        )
    return total


def shards(log_perm, panel, wells, rates, recharge, gauge):
    place = lax.axis_index("cell")
    parts = lax.axis_size("cell")
    slab, rows_y, depth_z = log_perm.shape
    cols = panel.shape[0]
    tests_here, well_count = wells.shape
    first, keeps, pushes = cheb_table(CHEB)
    reach = 2 * CHEB + 1
    rows_ext = slab + 2 * reach
    perm = jnp.exp(log_perm)
    scaled = perm[None] * panel
    stacked = jnp.concatenate([perm[None], scaled, recharge], axis=0)
    ext = with_halo(stacked, "cell", 1, reach)
    perm_ext = ext[0]
    scaled_ext = ext[1 : 1 + cols]
    rech_own = ext[1 + cols :]
    cells = slab * rows_y * depth_z
    packed = jnp.concatenate(
        [recharge.reshape(tests_here, cells), wells.astype(jnp.float32), rates], axis=1
    )
    groups = lax.axis_size("test")
    tests = groups * tests_here
    others = jnp.concatenate(
        [
            lax.ppermute(packed, "test", [(i, (i + shift) % groups) for i in range(groups)])
            for shift in range(1, groups)
        ]
        or [packed[:0]],
        axis=0,
    )
    rech_others = with_halo(
        others[:, :cells].reshape(tests - tests_here, slab, rows_y, depth_z), "cell", 1, reach
    )
    wells_others = others[:, cells : cells + well_count].astype(jnp.int32)
    rates_others = others[:, cells + well_count :]

    gx = place * slab - reach + jnp.arange(rows_ext, dtype=jnp.int32)
    mask_ext = ((gx >= 0) & (gx < parts * slab)).astype(jnp.float32)[:, None, None]
    flat = (
        gx[:, None, None] * (rows_y * depth_z)
        + jnp.arange(rows_y, dtype=jnp.int32)[None, :, None] * depth_z
        + jnp.arange(depth_z, dtype=jnp.int32)[None, None, :]
    )

    perm_faces = faces(perm_ext)

    def rows_of(field, halo):
        return lax.slice_in_dim(field, reach - halo, reach + slab + halo, axis=field.ndim - 3)

    iy = lax.broadcasted_iota(jnp.int32, (rows_y, depth_z), 0)
    iz = lax.broadcasted_iota(jnp.int32, (rows_y, depth_z), 1)
    face_stack = jnp.stack(
        [
            perm_faces[0],
            perm_faces[1],
            jnp.where(iy < rows_y - 1, perm_faces[2], 0.0),
            jnp.where(iy > 0, perm_faces[3], 0.0),
            jnp.where(iz < depth_z - 1, perm_faces[4], 0.0),
            jnp.where(iz > 0, perm_faces[5], 0.0),
            storage + (
                perm_faces[0] + perm_faces[1] + perm_faces[2]
                + perm_faces[3] + perm_faces[4] + perm_faces[5]
            ),
        ]
    ) * mask_ext[None, 1:-1]

    def solve(right_side, halo):
        lead = right_side.shape[:-3]
        flat_side = right_side.reshape((-1,) + right_side.shape[-3:])
        result = kernel_solve(
            flat_side, face_stack, reach - halo, first, keeps, pushes
        )
        return result.reshape(lead + result.shape[-3:]), halo - CHEB

    def begin(rech_ext, well_rows, rate_rows):
        hits = well_rows[:, :, None, None, None] == flat[None, None]
        points = jnp.sum(jnp.where(hits, rate_rows[:, :, None, None, None], 0.0), axis=1)
        own_hits = hits[:, :, reach : reach + slab]
        counts = jnp.sum(own_hits.astype(jnp.float32), axis=1)
        observe = gauge[None] + counts
        state, state_halo = solve(rech_ext + points, reach)
        forcing = -diffuse(rows_of(scaled_ext, state_halo)[None], state[:, None])
        forcing = forcing * rows_of(mask_ext, state_halo - 1)
        state = lax.slice_in_dim(state, CHEB, state.shape[1] - CHEB, axis=1)
        return state, forcing, observe

    parts_of = [begin(rech_own, wells, rates)]
    if tests > tests_here:
        parts_of.append(begin(rech_others, wells_others, rates_others))
    state, forcing, observe = (jnp.concatenate(group, axis=0) for group in zip(*parts_of))
    forcing = forcing.reshape(tests * cols, slab + 2 * CHEB, rows_y, depth_z)
    fields = tests * cols
    observe_fields = jnp.broadcast_to(
        observe[:, None], (tests, cols, slab, rows_y, depth_z)
    ).reshape(fields, slab, rows_y, depth_z)
    half = fields // 2
    spans = [(0, half), (half, fields)] if half else [(0, fields)]
    halos = []
    ahead = forcing[spans[0][0] : spans[0][1]]
    for index, (lo, hi) in enumerate(spans):
        change, _ = solve(ahead, CHEB)
        weighted = change * observe_fields[lo:hi]
        if index + 1 < len(spans):
            nxt = spans[index + 1]
            weighted, ahead = lax.optimization_barrier((weighted, forcing[nxt[0] : nxt[1]]))
        halos.append(with_halo(weighted, "cell", 1, CHEB + 1))
    adjoints = []
    for part in halos:
        adjoints.append(solve(part, CHEB + 1)[0])
    adjoint = jnp.concatenate(adjoints, axis=0)
    adjoint = adjoint.reshape(tests, cols, slab + 2, rows_y, depth_z)
    contrib = jnp.sum(pairs(state[:, None], adjoint), axis=0)
    return -0.5 * perm[None] * contrib


def solution(mesh):
    return jax.shard_map(
        shards,
        mesh=mesh,
        in_specs=(
            P("cell", None, None),
            P("test", "cell", None, None),
            P("test", None),
            P("test", None),
            P("test", "cell", None, None),
            P("cell", None, None),
        ),
        out_specs=P("test", "cell", None, None),
        check_vma=False,
    )
```

```python
import functools
import math

import jax
import jax.numpy as jnp
from jax import lax
from jax.experimental import pallas as pl
from jax.experimental.pallas import tpu as pltpu
from jax.sharding import PartitionSpec as P


CHEB = 4


storage = 0.02


def with_halo(cells, axis, dim, width):
    count = lax.axis_size(axis)
    ends = count - 1
    head = lax.slice_in_dim(cells, 0, width, axis=dim)
    tail = lax.slice_in_dim(cells, cells.shape[dim] - width, cells.shape[dim], axis=dim)
    return jnp.concatenate(
        [
            lax.ppermute(tail, axis, [(i, i + 1) for i in range(ends)]),
            cells,
            lax.ppermute(head, axis, [(i + 1, i) for i in range(ends)]),
        ],
        axis=dim,
    )


INTERPRET = False


def solve_kernel(b_ref, k_ref, o_ref, sol, res, da, db, *, offset, first, keeps, pushes):
    block, rows, rows_y, depth_z = sol.shape

    def init(r, c):
        da[:, r] = b_ref[:, r] * first
        return c

    lax.fori_loop(0, rows, init, 0, unroll=True)
    bufs = (da, db)
    for turn in range(CHEB):
        src = bufs[turn % 2]
        dst = bufs[(turn + 1) % 2]
        keep = keeps[turn]
        push = pushes[turn]

        def step(r, c, turn=turn, src=src, dst=dst, keep=keep, push=push):
            face = r - 1 + offset
            coeff = [k_ref[j, face] for j in range(7)]
            for f in range(block):
                here = src[f, r]
                image = coeff[6] * here - coeff[0] * src[f, r + 1]
                image = image - coeff[1] * src[f, r - 1]
                image = image - coeff[2] * pltpu.roll(here, rows_y - 1, 0)
                image = image - coeff[3] * pltpu.roll(here, 1, 0)
                image = image - coeff[4] * pltpu.roll(here, depth_z - 1, 1)
                image = image - coeff[5] * pltpu.roll(here, 1, 1)
                if turn == 0:
                    summed = here
                    fresh = b_ref[f, r] - image
                else:
                    summed = sol[f, r] + here
                    fresh = res[f, r] - image
                after = keep * here + push * fresh
                if turn == CHEB - 1:
                    o_ref[f, r - CHEB] = summed + after
                else:
                    sol[f, r] = summed
                    res[f, r] = fresh
                    dst[f, r] = after
            return c

        lax.fori_loop(turn + 1, rows - 1 - turn, step, 0, unroll=True)


def kernel_solve(right_side, face_stack, offset, first, keeps, pushes):
    fields, rows, rows_y, depth_z = right_side.shape
    block = 2 if fields % 2 == 0 else 1
    body = functools.partial(
        solve_kernel,
        offset=offset,
        first=first,
        keeps=tuple(keeps),
        pushes=tuple(pushes),
    )
    return pl.pallas_call(
        body,
        grid=(fields // block,),
        in_specs=[
            pl.BlockSpec((block, rows, rows_y, depth_z), lambda f: (f, 0, 0, 0)),
            pl.BlockSpec(face_stack.shape, lambda f: (0, 0, 0, 0)),
        ],
        out_specs=pl.BlockSpec((block, rows - 2 * CHEB, rows_y, depth_z), lambda f: (f, 0, 0, 0)),
        out_shape=jax.ShapeDtypeStruct((fields, rows - 2 * CHEB, rows_y, depth_z), jnp.float32),
        scratch_shapes=[
            pltpu.VMEM((block, rows, rows_y, depth_z), jnp.float32) for _ in range(4)
        ],
        compiler_params=pltpu.CompilerParams(vmem_limit_bytes=48 * 1024 * 1024),
        interpret=INTERPRET,
    )(right_side, face_stack)


def cheb_table(count):
    highest = storage + 12.0 * math.e
    theta = 0.5 * (highest + storage)
    spread = 0.5 * (highest - storage)
    sigma = theta / spread
    rho = 1.0 / sigma
    keeps = []
    pushes = []
    for _ in range(count):
        after = 1.0 / (2.0 * sigma - rho)
        keeps.append(after * rho)
        pushes.append(2.0 * after / spread)
        rho = after
    return (1.0 / theta, keeps, pushes)


def neighbours(field, back):
    axis = field.ndim - back
    widths = [(0, 0)] * field.ndim
    widths[axis] = (1, 1)
    padded = jnp.pad(field, widths)
    length = field.shape[axis]
    return (
        lax.slice_in_dim(padded, 2, length + 2, axis=axis),
        lax.slice_in_dim(padded, 0, length, axis=axis),
    )


def diffuse(weight_ext, field_ext):
    weight = weight_ext[..., 1:-1, :, :]
    field = field_ext[..., 1:-1, :, :]
    total = 0.5 * (weight + weight_ext[..., 2:, :, :]) * (field - field_ext[..., 2:, :, :])
    total = total + 0.5 * (weight + weight_ext[..., :-2, :, :]) * (
        field - field_ext[..., :-2, :, :]
    )
    for back in (2, 1):
        weight_up, weight_down = neighbours(weight, back)
        field_up, field_down = neighbours(field, back)
        total = (
            total
            + 0.5 * (weight + weight_up) * (field - field_up)
            + 0.5 * (weight + weight_down) * (field - field_down)
        )
    return total


def faces(weight_ext):
    weight = weight_ext[1:-1]
    weight_up_y, weight_down_y = neighbours(weight, 2)
    weight_up_z, weight_down_z = neighbours(weight, 1)
    return (
        0.5 * (weight + weight_ext[2:]),
        0.5 * (weight + weight_ext[:-2]),
        0.5 * (weight + weight_up_y),
        0.5 * (weight + weight_down_y),
        0.5 * (weight + weight_up_z),
        0.5 * (weight + weight_down_z),
    )


def pairs(left_ext, right_ext):
    left = left_ext[..., 1:-1, :, :]
    right = right_ext[..., 1:-1, :, :]
    total = (left - left_ext[..., 2:, :, :]) * (right - right_ext[..., 2:, :, :])
    total = total + (left - left_ext[..., :-2, :, :]) * (right - right_ext[..., :-2, :, :])
    for back in (2, 1):
        left_up, left_down = neighbours(left, back)
        right_up, right_down = neighbours(right, back)
        total = (
            total
            + (left - left_up) * (right - right_up)
            + (left - left_down) * (right - right_down)
        )
    return total


def shards(log_perm, panel, wells, rates, recharge, gauge):
    place = lax.axis_index("cell")
    parts = lax.axis_size("cell")
    slab, rows_y, depth_z = log_perm.shape
    cols = panel.shape[0]
    tests_here, well_count = wells.shape
    first, keeps, pushes = cheb_table(CHEB)
    reach = 2 * CHEB + 1
    rows_ext = slab + 2 * reach
    perm = jnp.exp(log_perm)
    scaled = perm[None] * panel
    stacked = jnp.concatenate([perm[None], scaled, recharge], axis=0)
    ext = with_halo(stacked, "cell", 1, reach)
    perm_ext = ext[0]
    scaled_ext = ext[1 : 1 + cols]
    rech_own = ext[1 + cols :]
    cells = slab * rows_y * depth_z
    packed = jnp.concatenate(
        [recharge.reshape(tests_here, cells), wells.astype(jnp.float32), rates], axis=1
    )
    groups = lax.axis_size("test")
    tests = groups * tests_here
    others = jnp.concatenate(
        [
            lax.ppermute(packed, "test", [(i, (i + shift) % groups) for i in range(groups)])
            for shift in range(1, groups)
        ]
        or [packed[:0]],
        axis=0,
    )
    rech_others = with_halo(
        others[:, :cells].reshape(tests - tests_here, slab, rows_y, depth_z), "cell", 1, reach
    )
    wells_others = others[:, cells : cells + well_count].astype(jnp.int32)
    rates_others = others[:, cells + well_count :]

    gx = place * slab - reach + jnp.arange(rows_ext, dtype=jnp.int32)
    mask_ext = ((gx >= 0) & (gx < parts * slab)).astype(jnp.float32)[:, None, None]
    flat = (
        gx[:, None, None] * (rows_y * depth_z)
        + jnp.arange(rows_y, dtype=jnp.int32)[None, :, None] * depth_z
        + jnp.arange(depth_z, dtype=jnp.int32)[None, None, :]
    )

    perm_faces = faces(perm_ext)

    def rows_of(field, halo):
        return lax.slice_in_dim(field, reach - halo, reach + slab + halo, axis=field.ndim - 3)

    iy = lax.broadcasted_iota(jnp.int32, (rows_y, depth_z), 0)
    iz = lax.broadcasted_iota(jnp.int32, (rows_y, depth_z), 1)
    face_stack = jnp.stack(
        [
            perm_faces[0],
            perm_faces[1],
            jnp.where(iy < rows_y - 1, perm_faces[2], 0.0),
            jnp.where(iy > 0, perm_faces[3], 0.0),
            jnp.where(iz < depth_z - 1, perm_faces[4], 0.0),
            jnp.where(iz > 0, perm_faces[5], 0.0),
            storage + (
                perm_faces[0] + perm_faces[1] + perm_faces[2]
                + perm_faces[3] + perm_faces[4] + perm_faces[5]
            ),
        ]
    ) * mask_ext[None, 1:-1]

    def solve(right_side, halo):
        lead = right_side.shape[:-3]
        flat_side = right_side.reshape((-1,) + right_side.shape[-3:])
        result = kernel_solve(
            flat_side,
            lax.slice_in_dim(face_stack, reach - halo, reach + slab + halo - 2, axis=1),
            0,
            first,
            keeps,
            pushes,
        )
        return result.reshape(lead + result.shape[-3:]), halo - CHEB

    def begin(rech_ext, well_rows, rate_rows):
        hits = well_rows[:, :, None, None, None] == flat[None, None]
        points = jnp.sum(jnp.where(hits, rate_rows[:, :, None, None, None], 0.0), axis=1)
        own_hits = hits[:, :, reach : reach + slab]
        counts = jnp.sum(own_hits.astype(jnp.float32), axis=1)
        observe = gauge[None] + counts
        state, state_halo = solve(rech_ext + points, reach)
        forcing = -diffuse(rows_of(scaled_ext, state_halo)[None], state[:, None])
        forcing = forcing * rows_of(mask_ext, state_halo - 1)
        state = lax.slice_in_dim(state, CHEB, state.shape[1] - CHEB, axis=1)
        return state, forcing, observe

    parts_of = [begin(rech_own, wells, rates)]
    if tests > tests_here:
        parts_of.append(begin(rech_others, wells_others, rates_others))
    state, forcing, observe = (jnp.concatenate(group, axis=0) for group in zip(*parts_of))
    forcing = forcing.reshape(tests * cols, slab + 2 * CHEB, rows_y, depth_z)
    fields = tests * cols
    observe_fields = jnp.broadcast_to(
        observe[:, None], (tests, cols, slab, rows_y, depth_z)
    ).reshape(fields, slab, rows_y, depth_z)
    half = fields // 2
    spans = [(0, half), (half, fields)] if half else [(0, fields)]
    halos = []
    ahead = forcing[spans[0][0] : spans[0][1]]
    for index, (lo, hi) in enumerate(spans):
        change, _ = solve(ahead, CHEB)
        weighted = change * observe_fields[lo:hi]
        if index + 1 < len(spans):
            nxt = spans[index + 1]
            weighted, ahead = lax.optimization_barrier((weighted, forcing[nxt[0] : nxt[1]]))
        halos.append(with_halo(weighted, "cell", 1, CHEB + 1))
    adjoints = []
    for part in halos:
        adjoints.append(solve(part, CHEB + 1)[0])
    adjoint = jnp.concatenate(adjoints, axis=0)
    adjoint = adjoint.reshape(tests, cols, slab + 2, rows_y, depth_z)
    contrib = jnp.sum(pairs(state[:, None], adjoint), axis=0)
    return -0.5 * perm[None] * contrib


def solution(mesh):
    return jax.shard_map(
        shards,
        mesh=mesh,
        in_specs=(
            P("cell", None, None),
            P("test", "cell", None, None),
            P("test", None),
            P("test", None),
            P("test", "cell", None, None),
            P("cell", None, None),
        ),
        out_specs=P("test", "cell", None, None),
        check_vma=False,
    )
```
